32 devices in a mesh: ctx: 8 (over z, x), head: 4 (over y, core).
Axes of the slice: x: 2, y: 2, z: 4, core: 2. Of those that a mesh axis runs over, the one named last changes fastest.
Arguments:
- queries: bfloat16 [4096, 2048], P('ctx', 'head'), may hold values from -50 to 50
- keys: bfloat16 [4096, 2048], P('ctx', 'head'), may hold values from -4 to 4
- values: bfloat16 [4096, 2048], P('ctx', 'head'), may hold values from -6 to 6
- out_weight: bfloat16 [2048, 2048], P('head'), may hold values from -0.125 to 0.125
- d_out: bfloat16 [4096, 2048], P('ctx', 'head'), may hold values from -6 to 6
- window: int32 [32], replicated, may hold values from 0 to 3
- far_select: int32 [32, 5], replicated, may hold values 0 or 1
Outputs:
- output: bfloat16 [4096, 2048], P('ctx', 'head')
- d_queries: bfloat16 [4096, 2048], P('ctx', 'head')
- d_keys: bfloat16 [4096, 2048], P('ctx', 'head')
- d_values: bfloat16 [4096, 2048], P('ctx', 'head')
The draws below stay inside these ranges and needn't reach their ends.
All inputs are finite; a program needn't handle non-finite values.
Results may differ from the reference program's by a relative error of at most 0.04.
Values may be sent and summed in bfloat16 or wider, within the bound.
No kernel may reach another device: no remote copies, remote signals or barrier semaphores. Data moves between devices by JAX's collectives and lax.ppermute only.
A program may use at most 128 MiB of HBM per device.

```python
import jax
import jax.numpy as jnp
from jax import lax

D = 2048
HEADS = 16
HD = 128
BLK = 128
WIN_MAX = 3
LEVELS = 5
NB = 4
NBLK = 32
TOKENS = 4096


def key_sample(key):
    sub_key = jax.random.fold_in(key, 11)
    sample = jnp.clip(jax.random.normal(sub_key, (TOKENS, HEADS * HD), jnp.float32), -4.0, 4.0)
    return sample


def draw_keys(key, part):
    sample = key_sample(key)
    return sample.astype(jnp.bfloat16)


def draw_queries(key, part):
    sub_key = jax.random.fold_in(key, 23)
    sample = jnp.clip(2.0 * jax.random.normal(sub_key, (TOKENS, HEADS * HD), jnp.float32), -8.0, 8.0)
    return sample.astype(jnp.bfloat16)


def place_ends(entries, rng, low, top_value):
    dims = entries.shape
    place = [jax.random.randint(jax.random.fold_in(rng, axis), (), 0, dims[axis]) for axis in range(len(dims))]
    entries = entries.at[tuple(place)].set(low)
    longest = dims.index(max(dims))
    place[longest] = (place[longest] + 1) % dims[longest]
    return entries.at[tuple(place)].set(top_value)


def level_of(stream_key, dims, cuts, low, top_value):
    level = 1.0
    for dim, shards_of in cuts:
        heights = jax.random.uniform(jax.random.fold_in(jax.random.fold_in(stream_key, 6), dim), (shards_of,), jnp.float32, low / len(cuts), top_value / len(cuts))
        level = level * jnp.repeat(jnp.exp(heights), dims[dim] // shards_of).reshape((-1,) + (1,) * (len(dims) - 1 - dim))
    return level


def gaussian(stream_key, extent, scale, most, split=(), kind=jnp.bfloat16):
    array = jax.random.normal(stream_key, extent, jnp.float32) * scale
    if len(split) > 0:
        array = level_of(stream_key, extent, split, -0.22, 0.18) * array
    return jnp.clip(array, min=-most, max=most).astype(kind)


def setup_inputs(seed: int = 0) -> dict:
    streams_of = jax.random.split(jax.random.key(seed), 8)
    queries = draw_queries(jax.random.fold_in(streams_of[7], 71), 0)
    keys = draw_keys(jax.random.fold_in(streams_of[7], 71), 0)
    values = gaussian(streams_of[2], (TOKENS, HEADS * HD), 1.0, 6.0, ((0, 8), (1, 4)))
    out_weight = gaussian(streams_of[3], (HEADS * HD, D), (HEADS * HD) ** -0.5, 0.125, ((0, 4),))
    d_out = gaussian(streams_of[4], (TOKENS, D), 1.0, 6.0, ((0, 8), (1, 4)))
    window = place_ends(jax.random.randint(streams_of[5], (NBLK,), 0, WIN_MAX + 1), jax.random.fold_in(streams_of[5], 1), 0, WIN_MAX).astype(jnp.int32)
    far_select = place_ends((jax.random.randint(streams_of[6], (NBLK, LEVELS), 0, 2) < 1).astype(jnp.int32), jax.random.fold_in(streams_of[6], 1), 0, 1)
    return dict(queries=queries, keys=keys, values=values, out_weight=out_weight, d_out=d_out, window=window, far_select=far_select)


neg_large = -1.0e30


def full_mask(valid, block_width, diag_first):
    grid_shape = (block_width, valid.shape[1], block_width)
    query_pos = lax.broadcasted_iota(jnp.int32, grid_shape, 0)
    key_pos = lax.broadcasted_iota(jnp.int32, grid_shape, 2)
    candidate = lax.broadcasted_iota(jnp.int32, grid_shape, 1)
    inside = ((key_pos <= query_pos) | (candidate > 0)) if diag_first else (key_pos >= 0)
    return valid[:, None, None, :, None] & inside[None, None]


def scores_of(queries, keys, allowed):
    score_scale = queries.shape[-1] ** -0.5
    raw_scores = jnp.einsum("nqhe,nckhe->nhqck", queries.astype(jnp.float32), keys.astype(jnp.float32)) * score_scale
    return jnp.where(allowed, raw_scores, neg_large)


def attend(queries, keys, values, allowed):
    scores = scores_of(queries, keys, allowed)
    row_max = jnp.max(scores, axis=(3, 4), keepdims=True)
    row_total = jnp.sum(jnp.exp(scores - row_max), axis=(3, 4), keepdims=True)
    log_total = row_max + jnp.log(row_total)
    weights = jnp.exp(scores - log_total).astype(jnp.bfloat16)
    attended = jnp.einsum("nhqck,nckhe->nqhe", weights.astype(jnp.float32), values.astype(jnp.float32))
    return attended.astype(jnp.bfloat16), log_total[:, :, :, 0, 0]


def attend_grads(queries, d_att, log_total, delta, keys, values, allowed):
    score_scale = queries.shape[-1] ** -0.5
    scores = scores_of(queries, keys, allowed)
    probabilities = jnp.exp(scores - log_total[:, :, :, None, None])
    weights = probabilities.astype(jnp.bfloat16)
    value_grad = jnp.einsum("nhqck,nqhe->nckhe", weights.astype(jnp.float32), d_att.astype(jnp.float32))
    d_prob = jnp.einsum("nqhe,nckhe->nhqck", d_att.astype(jnp.float32), values.astype(jnp.float32))
    d_score = (probabilities * (d_prob - delta[:, :, :, None, None]) * score_scale).astype(jnp.bfloat16)
    query_grad = jnp.einsum("nhqck,nckhe->nqhe", d_score.astype(jnp.float32), keys.astype(jnp.float32))
    key_grad = jnp.einsum("nhqck,nqhe->nckhe", d_score.astype(jnp.float32), queries.astype(jnp.float32))
    return query_grad, key_grad, value_grad


def row_delta(d_att, attended):
    summed = jnp.sum(d_att.astype(jnp.float32) * attended.astype(jnp.float32), axis=3)
    return jnp.transpose(summed, (0, 2, 1))


def reference(queries, keys, values, out_weight, d_out, window, far_select):
    token_count = queries.shape[0]
    nblocks = token_count // BLK
    block_ids = jnp.arange(nblocks, dtype=jnp.int32)
    offsets = [0] + list(range(1, WIN_MAX + 1)) + [NB * 2 ** exponent for exponent in range(LEVELS)]
    valid_cols = [block_ids >= 0]
    for offset in range(1, WIN_MAX + 1):
        valid_cols.append((offset <= window) & (block_ids - offset >= 0))
    for exponent in range(LEVELS):
        valid_cols.append((far_select[:, exponent] == 1) & (block_ids - NB * 2 ** exponent >= 0))
    valid = jnp.stack(valid_cols, axis=1)
    source_index = jnp.stack([jnp.maximum(block_ids - offset, 0).astype(jnp.int32) for offset in offsets], axis=1)
    allowed = full_mask(valid, BLK, True)
    cand_count = len(offsets)
    grad_att = jnp.dot(d_out, out_weight.T, preferred_element_type=jnp.float32).astype(jnp.bfloat16)

    def per_head(head_index):
        start = (head_index * HD).astype(jnp.int32)
        query_head = lax.dynamic_slice_in_dim(queries, start, HD, 1).reshape(nblocks, BLK, 1, HD)
        key_head = lax.dynamic_slice_in_dim(keys, start, HD, 1).reshape(nblocks, BLK, 1, HD)
        value_head = lax.dynamic_slice_in_dim(values, start, HD, 1).reshape(nblocks, BLK, 1, HD)
        grad_head = lax.dynamic_slice_in_dim(grad_att, start, HD, 1).reshape(nblocks, BLK, 1, HD)
        cand_keys = key_head[source_index]
        cand_values = value_head[source_index]
        attended, log_total = attend(query_head, cand_keys, cand_values, allowed)
        delta = row_delta(grad_head, attended)
        query_grad, key_grad, value_grad = attend_grads(query_head, grad_head, log_total, delta, cand_keys, cand_values, allowed)
        flat_index = source_index.reshape(-1)
        key_sum = jax.ops.segment_sum(key_grad.reshape(nblocks * cand_count, BLK, 1, HD), flat_index, num_segments=nblocks)
        value_sum = jax.ops.segment_sum(value_grad.reshape(nblocks * cand_count, BLK, 1, HD), flat_index, num_segments=nblocks)
        return (attended, query_grad.astype(jnp.bfloat16), key_sum.astype(jnp.bfloat16), value_sum.astype(jnp.bfloat16))

    stacked = lax.map(per_head, jnp.arange(HEADS, dtype=jnp.int32))

    def merge_heads(per_heads):
        return jnp.transpose(per_heads[:, :, :, 0, :], (1, 2, 0, 3)).reshape(token_count, HEADS * HD)

    attended_all = merge_heads(stacked[0])
    output = jnp.dot(attended_all, out_weight, preferred_element_type=jnp.float32).astype(jnp.bfloat16)
    return (output, merge_heads(stacked[1]), merge_heads(stacked[2]), merge_heads(stacked[3]))
```

```python
import jax
import jax.numpy as jnp
from jax import lax
from jax.sharding import PartitionSpec as P

HD = 128
BLK = 128
WIN_MAX = 3
LEVELS = 5
NB = 4


neg_large = -1e30


def passed_along(block, axis, distance):
    devices = range(lax.axis_size(axis))
    route = [(i - distance, i) for i in devices if i - distance in devices]
    return lax.ppermute(block, axis, route)


def causal_first(valid):
    grid_shape = (BLK, valid.shape[1], BLK)
    query_pos = lax.broadcasted_iota(jnp.int32, grid_shape, 0)
    key_pos = lax.broadcasted_iota(jnp.int32, grid_shape, 2)
    candidate = lax.broadcasted_iota(jnp.int32, grid_shape, 1)
    inside = (key_pos <= query_pos) | (candidate > 0)
    return valid[:, None, None, :, None] & inside[None, None]


def causal_first_keyside(valid):
    grid_shape = (valid.shape[1], BLK, BLK)
    candidate = lax.broadcasted_iota(jnp.int32, grid_shape, 0)
    query_pos = lax.broadcasted_iota(jnp.int32, grid_shape, 1)
    key_pos = lax.broadcasted_iota(jnp.int32, grid_shape, 2)
    inside = (key_pos <= query_pos) | (candidate > 0)
    return valid[:, None, :, None, None] & inside[None, None]


def query_side(q, g, cand_k, cand_v, allowed):
    scale = HD ** (-0.5)
    raw = jnp.einsum("nqhe,nckhe->nhqck", q, cand_k, preferred_element_type=jnp.float32) * scale
    scores = jnp.where(allowed, raw, neg_large)
    row_max = jnp.max(scores, axis=(3, 4), keepdims=True)
    row_total = jnp.sum(jnp.exp(scores - row_max), axis=(3, 4), keepdims=True)
    log_total = row_max + jnp.log(row_total)
    probabilities = jnp.exp(scores - log_total)
    weights = probabilities.astype(jnp.bfloat16)
    attended = jnp.einsum(
        "nhqck,nckhe->nqhe", weights, cand_v, preferred_element_type=jnp.float32
    ).astype(jnp.bfloat16)
    delta = jnp.transpose(
        jnp.sum(g.astype(jnp.float32) * attended.astype(jnp.float32), axis=3), (0, 2, 1)
    )
    d_prob = jnp.einsum("nqhe,nckhe->nhqck", g, cand_v, preferred_element_type=jnp.float32)
    d_score = (probabilities * (d_prob - delta[:, :, :, None, None]) * scale).astype(jnp.bfloat16)
    query_grad = jnp.einsum("nhqck,nckhe->nqhe", d_score, cand_k, preferred_element_type=jnp.float32)
    return attended, log_total[:, :, :, 0, 0], delta, query_grad


def key_side(k, v, cand_q, cand_g, cand_lse, cand_delta, allowed):
    scale = HD ** (-0.5)
    raw = jnp.einsum("ncqhe,nkhe->nhcqk", cand_q, k, preferred_element_type=jnp.float32) * scale
    scores = jnp.where(allowed, raw, neg_large)
    lse = jnp.transpose(cand_lse, (0, 2, 1, 3))[..., None]
    delta = jnp.transpose(cand_delta, (0, 2, 1, 3))[..., None]
    probabilities = jnp.exp(scores - lse)
    weights = probabilities.astype(jnp.bfloat16)
    value_grad = jnp.einsum("nhcqk,ncqhe->nkhe", weights, cand_g, preferred_element_type=jnp.float32)
    d_prob = jnp.einsum("ncqhe,nkhe->nhcqk", cand_g, v, preferred_element_type=jnp.float32)
    d_score = (probabilities * (d_prob - delta) * scale).astype(jnp.bfloat16)
    key_grad = jnp.einsum("nhcqk,ncqhe->nkhe", d_score, cand_q, preferred_element_type=jnp.float32)
    return key_grad, value_grad


def local(queries, keys, values, out_weight, d_out, window, far_select):
    tokens_local = queries.shape[0]
    heads_local = queries.shape[1] // HD
    assert tokens_local == NB * BLK
    ctx_count = lax.axis_size("ctx")
    ctx_index = lax.axis_index("ctx")
    nblocks = ctx_count * NB
    block_shape = (NB, BLK, heads_local, HD)
    q = queries.reshape(block_shape)
    k = keys.reshape(block_shape)
    v = values.reshape(block_shape)
    local_ids = jnp.arange(NB, dtype=jnp.int32)
    block_ids = ctx_index * NB + local_ids
    levels = [m for m in range(LEVELS) if 2**m < ctx_count]

    from_below = {m: passed_along((k, v), "ctx", 2**m) for m in levels}
    q_above = {m: passed_along(q, "ctx", -(2**m)) for m in levels}

    grad_att = lax.dot_general(
        lax.all_gather(d_out, "head", axis=1, tiled=True),
        out_weight,
        (((1,), (1,)), ((), ())),
        preferred_element_type=jnp.float32,
    )
    g = grad_att.astype(jnp.bfloat16).reshape(block_shape)
    g_above = {m: passed_along(g, "ctx", -(2**m)) for m in levels}

    prev_k, prev_v = from_below[0]
    ext_k = jnp.concatenate([prev_k, k], axis=0)
    ext_v = jnp.concatenate([prev_v, v], axis=0)
    cand_k = jnp.stack(
        [k]
        + [ext_k[NB - o : 2 * NB - o] for o in range(1, WIN_MAX + 1)]
        + [from_below[m][0] for m in levels],
        axis=1,
    )
    cand_v = jnp.stack(
        [v]
        + [ext_v[NB - o : 2 * NB - o] for o in range(1, WIN_MAX + 1)]
        + [from_below[m][1] for m in levels],
        axis=1,
    )
    own_window = lax.dynamic_slice_in_dim(window, ctx_index * NB, NB, 0)
    own_select = lax.dynamic_slice_in_dim(far_select, ctx_index * NB, NB, 0)
    valid_cols = [block_ids >= 0]
    for offset in range(1, WIN_MAX + 1):
        valid_cols.append((offset <= own_window) & (block_ids - offset >= 0))
    for m in levels:
        valid_cols.append((own_select[:, m] == 1) & (block_ids - NB * 2**m >= 0))
    allowed_q = causal_first(jnp.stack(valid_cols, axis=1))
    attended, log_total, delta, query_grad = query_side(q, g, cand_k, cand_v, allowed_q)

    attended_flat = attended.reshape(tokens_local, heads_local * HD)
    partial_out = jnp.dot(attended_flat, out_weight, preferred_element_type=jnp.float32)
    output = lax.psum_scatter(
        partial_out.astype(jnp.bfloat16), "head", scatter_dimension=1, tiled=True
    )

    stats_above = {m: passed_along((log_total, delta), "ctx", -(2**m)) for m in levels}

    def key_candidates(own, above):
        ext = jnp.concatenate([own, above[0]], axis=0)
        return jnp.stack(
            [own] + [ext[o : o + NB] for o in range(1, WIN_MAX + 1)] + [above[m] for m in levels],
            axis=1,
        )

    cand_q = key_candidates(q, q_above)
    cand_g = key_candidates(g, g_above)
    cand_lse = key_candidates(log_total, {m: stats_above[m][0] for m in levels})
    cand_delta = key_candidates(delta, {m: stats_above[m][1] for m in levels})
    last = nblocks - 1
    key_cols = [block_ids >= 0]
    for offset in range(1, WIN_MAX + 1):
        qb = block_ids + offset
        key_cols.append((qb <= last) & (offset <= jnp.take(window, jnp.minimum(qb, last))))
    for m in levels:
        qb = block_ids + NB * 2**m
        key_cols.append((qb <= last) & (jnp.take(far_select[:, m], jnp.minimum(qb, last)) == 1))
    allowed_k = causal_first_keyside(jnp.stack(key_cols, axis=1))
    key_grad, value_grad = key_side(k, v, cand_q, cand_g, cand_lse, cand_delta, allowed_k)

    flat_shape = (tokens_local, heads_local * HD)
    return (
        output,
        query_grad.reshape(flat_shape).astype(jnp.bfloat16),
        key_grad.reshape(flat_shape).astype(jnp.bfloat16),
        value_grad.reshape(flat_shape).astype(jnp.bfloat16),
    )


def solution(mesh):
    return jax.shard_map(
        local,
        mesh=mesh,
        in_specs=(
            P("ctx", "head"),
            P("ctx", "head"),
            P("ctx", "head"),
            P("head", None),
            P("ctx", "head"),
            P(),
            P(),
        ),
        out_specs=(P("ctx", "head"), P("ctx", "head"), P("ctx", "head"), P("ctx", "head")),
        check_vma=False,
    )
```

```python
import functools

import jax
import jax.numpy as jnp
from jax import lax
from jax.experimental import pallas as pl
from jax.experimental.pallas import tpu as pltpu
from jax.sharding import PartitionSpec as P

HD = 128
BLK = 128
WIN_MAX = 3
LEVELS = 5
NB = 4


neg_large = -1e30


def passed_along(block, axis, distance):
    devices = range(lax.axis_size(axis))
    route = [(i - distance, i) for i in devices if i - distance in devices]
    return lax.ppermute(block, axis, route)


def dot_nt(a, b):
    return lax.dot_general(a, b, (((1,), (1,)), ((), ())), preferred_element_type=jnp.float32)


def dot_nn(a, b):
    return jnp.dot(a, b, preferred_element_type=jnp.float32)


def col_to_row(col):
    eye = lax.broadcasted_iota(jnp.int32, (BLK, BLK), 0) == lax.broadcasted_iota(
        jnp.int32, (BLK, BLK), 1
    )
    return jnp.sum(jnp.where(eye, col, 0.0), axis=0, keepdims=True)


def query_kernel(n_levels, valid_ref, q_ref, g_ref, k_ref, v_ref, *rest):
    kf = rest[0 : 2 * n_levels : 2]
    vf = rest[1 : 2 * n_levels : 2]
    att_ref, dq_ref, st_ref = rest[2 * n_levels :]
    n_cand = 1 + WIN_MAX + n_levels
    scale = HD ** (-0.5)
    causal = lax.broadcasted_iota(jnp.int32, (BLK, BLK), 1) <= lax.broadcasted_iota(
        jnp.int32, (BLK, BLK), 0
    )
    for n in range(NB):
        rows = pl.ds(n * BLK, BLK)
        qn = q_ref[rows, :]
        gn = g_ref[rows, :]
        cands = [(k_ref, v_ref, n)]
        for o in range(1, WIN_MAX + 1):
            j = n - o
            cands.append((k_ref, v_ref, j) if j >= 0 else (kf[0], vf[0], NB + j))
        for mi in range(n_levels):
            cands.append((kf[mi], vf[mi], n))
        scores = []
        for ci, (kr, _, j) in enumerate(cands):
            s = dot_nt(qn, kr[pl.ds(j * BLK, BLK), :]) * scale
            if ci == 0:
                s = jnp.where(causal, s, neg_large)
            else:
                s = jnp.where(valid_ref[n * n_cand + ci] != 0, s, neg_large)
            scores.append(s)
        row_max = scores[0].max(axis=1, keepdims=True)
        for s in scores[1:]:
            row_max = jnp.maximum(row_max, s.max(axis=1, keepdims=True))
        row_total = None
        for s in scores:
            part = jnp.sum(jnp.exp(s - row_max), axis=1, keepdims=True)
            row_total = part if row_total is None else row_total + part
        log_total = row_max + jnp.log(row_total)
        probs = [jnp.exp(s - log_total) for s in scores]
        att = None
        for p, (_, vr, j) in zip(probs, cands):
            part = dot_nn(p.astype(jnp.bfloat16), vr[pl.ds(j * BLK, BLK), :])
            att = part if att is None else att + part
        att_b = att.astype(jnp.bfloat16)
        att_ref[rows, :] = att_b
        delta = jnp.sum(gn.astype(jnp.float32) * att_b.astype(jnp.float32), axis=1, keepdims=True)
        dq = None
        for p, (kr, vr, j) in zip(probs, cands):
            d_prob = dot_nt(gn, vr[pl.ds(j * BLK, BLK), :])
            d_score = (p * (d_prob - delta) * scale).astype(jnp.bfloat16)
            part = dot_nn(d_score, kr[pl.ds(j * BLK, BLK), :])
            dq = part if dq is None else dq + part
        dq_ref[rows, :] = dq.astype(jnp.bfloat16)
        st_ref[0, 0, pl.ds(n, 1), :] = col_to_row(log_total)
        st_ref[1, 0, pl.ds(n, 1), :] = col_to_row(delta)


def key_kernel(n_levels, valid_ref, k_ref, v_ref, q_ref, g_ref, st_ref, *rest):
    qf = rest[0 : 3 * n_levels : 3]
    gf = rest[1 : 3 * n_levels : 3]
    sf = rest[2 : 3 * n_levels : 3]
    dk_ref, dv_ref = rest[3 * n_levels :]
    n_cand = 1 + WIN_MAX + n_levels
    scale = HD ** (-0.5)
    causal = lax.broadcasted_iota(jnp.int32, (BLK, BLK), 0) <= lax.broadcasted_iota(
        jnp.int32, (BLK, BLK), 1
    )
    for j in range(NB):
        rows = pl.ds(j * BLK, BLK)
        kj = k_ref[rows, :]
        vj = v_ref[rows, :]
        cands = [(q_ref, g_ref, st_ref, j)]
        for o in range(1, WIN_MAX + 1):
            i = j + o
            cands.append((q_ref, g_ref, st_ref, i) if i < NB else (qf[0], gf[0], sf[0], i - NB))
        for mi in range(n_levels):
            cands.append((qf[mi], gf[mi], sf[mi], j))
        dk = None
        dv = None
        for ci, (qr, gr, sr, i) in enumerate(cands):
            qc = qr[pl.ds(i * BLK, BLK), :]
            gc = gr[pl.ds(i * BLK, BLK), :]
            lse = sr[0, 0, pl.ds(i, 1), :]
            delta = sr[1, 0, pl.ds(i, 1), :]
            s = dot_nt(kj, qc) * scale
            if ci == 0:
                s = jnp.where(causal, s, neg_large)
            else:
                s = jnp.where(valid_ref[j * n_cand + ci] != 0, s, neg_large)
            p = jnp.exp(s - lse)
            part_v = dot_nn(p.astype(jnp.bfloat16), gc)
            d_prob = dot_nt(vj, gc)
            d_score = (p * (d_prob - delta) * scale).astype(jnp.bfloat16)
            part_k = dot_nn(d_score, qc)
            dv = part_v if dv is None else dv + part_v
            dk = part_k if dk is None else dk + part_k
        dk_ref[rows, :] = dk.astype(jnp.bfloat16)
        dv_ref[rows, :] = dv.astype(jnp.bfloat16)


def head_block(part):
    return pl.BlockSpec((NB * BLK, HD), lambda h, valid: (part, h))


def stats_block(heads):
    return pl.BlockSpec((2, 1, NB, BLK), lambda h, valid: (0, h, 0, 0))


def query_call(valid, q, g, k, v, kv_from, heads, n_levels):
    tokens, features = q.shape
    in_specs = [head_block(0)] * 4
    args = [q, g, k, v]
    for kv in kv_from:
        in_specs += [head_block(0), head_block(1)]
        args += [kv, kv]
    grid_spec = pltpu.PrefetchScalarGridSpec(
        num_scalar_prefetch=1,
        grid=(heads,),
        in_specs=in_specs,
        out_specs=[head_block(0), head_block(0), stats_block(heads)],
    )
    return pl.pallas_call(
        functools.partial(query_kernel, n_levels),
        grid_spec=grid_spec,
        out_shape=[
            jax.ShapeDtypeStruct((tokens, features), jnp.bfloat16),
            jax.ShapeDtypeStruct((tokens, features), jnp.bfloat16),
            jax.ShapeDtypeStruct((2, heads, NB, BLK), jnp.float32),
        ],
        name="query_side",
    )(valid, *args)


def key_call(valid, k, v, q, g, stats, qg_from, st_from, heads, n_levels):
    tokens, features = q.shape
    in_specs = [head_block(0)] * 4 + [stats_block(heads)]
    args = [k, v, q, g, stats]
    for qg, st in zip(qg_from, st_from):
        in_specs += [head_block(0), head_block(1), stats_block(heads)]
        args += [qg, qg, st]
    grid_spec = pltpu.PrefetchScalarGridSpec(
        num_scalar_prefetch=1,
        grid=(heads,),
        in_specs=in_specs,
        out_specs=[head_block(0), head_block(0)],
    )
    return pl.pallas_call(
        functools.partial(key_kernel, n_levels),
        grid_spec=grid_spec,
        out_shape=[
            jax.ShapeDtypeStruct((tokens, features), jnp.bfloat16),
            jax.ShapeDtypeStruct((tokens, features), jnp.bfloat16),
        ],
        name="key_side",
    )(valid, *args)


def local(queries, keys, values, out_weight, d_out, window, far_select):
    tokens_local = queries.shape[0]
    heads_local = queries.shape[1] // HD
    assert tokens_local == NB * BLK
    ctx_count = lax.axis_size("ctx")
    ctx_index = lax.axis_index("ctx")
    nblocks = ctx_count * NB
    last = nblocks - 1
    levels = [m for m in range(LEVELS) if 2**m < ctx_count]
    n_levels = len(levels)
    block_ids = ctx_index * NB + jnp.arange(NB, dtype=jnp.int32)

    kv = jnp.concatenate([keys, values], axis=0)
    kv_from = [passed_along(kv, "ctx", 2**m) for m in levels]

    grad_att = lax.dot_general(
        lax.all_gather(d_out, "head", axis=1, tiled=True),
        out_weight,
        (((1,), (1,)), ((), ())),
        preferred_element_type=jnp.float32,
    )
    g = grad_att.astype(jnp.bfloat16)
    qg = jnp.concatenate([queries, g], axis=0)
    qg_from = [passed_along(qg, "ctx", -(2**m)) for m in levels]

    own_window = lax.dynamic_slice_in_dim(window, ctx_index * NB, NB, 0)
    own_select = lax.dynamic_slice_in_dim(far_select, ctx_index * NB, NB, 0)
    valid_cols = [block_ids >= 0]
    for offset in range(1, WIN_MAX + 1):
        valid_cols.append((offset <= own_window) & (block_ids - offset >= 0))
    for m in levels:
        valid_cols.append((own_select[:, m] == 1) & (block_ids - NB * 2**m >= 0))
    valid_q = jnp.stack(valid_cols, axis=1).astype(jnp.int32).reshape(-1)

    key_cols = [block_ids >= 0]
    for offset in range(1, WIN_MAX + 1):
        qb = block_ids + offset
        key_cols.append((qb <= last) & (offset <= jnp.take(window, jnp.minimum(qb, last))))
    for m in levels:
        qb = block_ids + NB * 2**m
        key_cols.append((qb <= last) & (jnp.take(far_select[:, m], jnp.minimum(qb, last)) == 1))
    valid_k = jnp.stack(key_cols, axis=1).astype(jnp.int32).reshape(-1)

    attended, query_grad, stats = query_call(
        valid_q, queries, g, keys, values, kv_from, heads_local, n_levels
    )
    partial_out = jnp.dot(attended, out_weight, preferred_element_type=jnp.float32)
    output = lax.psum_scatter(
        partial_out.astype(jnp.bfloat16), "head", scatter_dimension=1, tiled=True
    )

    st_from = [passed_along(stats, "ctx", -(2**m)) for m in levels]
    key_grad, value_grad = key_call(
        valid_k, keys, values, queries, g, stats, qg_from, st_from, heads_local, n_levels
    )
    return output, query_grad, key_grad, value_grad


def solution(mesh):
    return jax.shard_map(
        local,
        mesh=mesh,
        in_specs=(
            P("ctx", "head"),
            P("ctx", "head"),
            P("ctx", "head"),
            P("head", None),
            P("ctx", "head"),
            P(),
            P(),
        ),
        out_specs=(P("ctx", "head"), P("ctx", "head"), P("ctx", "head"), P("ctx", "head")),
        check_vma=False,
    )
```

```python
import functools

import jax
import jax.numpy as jnp
from jax import lax
from jax.experimental import pallas as pl
from jax.experimental.pallas import tpu as pltpu
from jax.sharding import PartitionSpec as P

HD = 128
BLK = 128
WIN_MAX = 3
LEVELS = 5
NB = 4


neg_large = -1e30


def passed_along(block, axis, distance):
    devices = range(lax.axis_size(axis))
    route = [(i - distance, i) for i in devices if i - distance in devices]
    return lax.ppermute(block, axis, route)


def dot_nt(a, b):
    return lax.dot_general(a, b, (((1,), (1,)), ((), ())), preferred_element_type=jnp.float32)


def dot_nn(a, b):
    return jnp.dot(a, b, preferred_element_type=jnp.float32)


def col_to_row(col):
    eye = lax.broadcasted_iota(jnp.int32, (BLK, BLK), 0) == lax.broadcasted_iota(
        jnp.int32, (BLK, BLK), 1
    )
    return jnp.sum(jnp.where(eye, col, 0.0), axis=0, keepdims=True)


def query_kernel(n_levels, valid_ref, q_ref, g_ref, k_ref, v_ref, *rest):
    kf = rest[0 : 2 * n_levels : 2]
    vf = rest[1 : 2 * n_levels : 2]
    att_ref, dq_ref, st_ref = rest[2 * n_levels :]
    n_cand = 1 + WIN_MAX + n_levels
    scale = HD ** (-0.5)
    causal = lax.broadcasted_iota(jnp.int32, (BLK, BLK), 1) <= lax.broadcasted_iota(
        jnp.int32, (BLK, BLK), 0
    )
    for n in range(NB):
        rows = pl.ds(n * BLK, BLK)
        qn = q_ref[rows, :]
        gn = g_ref[rows, :]
        cands = [(k_ref, v_ref, n)]
        for o in range(1, WIN_MAX + 1):
            j = n - o
            cands.append((k_ref, v_ref, j) if j >= 0 else (kf[0], vf[0], NB + j))
        for mi in range(n_levels):
            cands.append((kf[mi], vf[mi], n))
        scores = []
        for ci, (kr, _, j) in enumerate(cands):
            s = dot_nt(qn, kr[pl.ds(j * BLK, BLK), :]) * scale
            if ci == 0:
                s = jnp.where(causal, s, neg_large)
            else:
                s = jnp.where(valid_ref[n * n_cand + ci] != 0, s, neg_large)
            scores.append(s)
        row_max = scores[0].max(axis=1, keepdims=True)
        for s in scores[1:]:
            row_max = jnp.maximum(row_max, s.max(axis=1, keepdims=True))
        row_total = None
        for s in scores:
            part = jnp.sum(jnp.exp(s - row_max), axis=1, keepdims=True)
            row_total = part if row_total is None else row_total + part
        log_total = row_max + jnp.log(row_total)
        probs = [jnp.exp(s - log_total) for s in scores]
        att = None
        for p, (_, vr, j) in zip(probs, cands):
            part = dot_nn(p.astype(jnp.bfloat16), vr[pl.ds(j * BLK, BLK), :])
            att = part if att is None else att + part
        att_b = att.astype(jnp.bfloat16)
        att_ref[rows, :] = att_b
        delta = jnp.sum(gn.astype(jnp.float32) * att_b.astype(jnp.float32), axis=1, keepdims=True)
        dq = None
        for p, (kr, vr, j) in zip(probs, cands):
            d_prob = dot_nt(gn, vr[pl.ds(j * BLK, BLK), :])
            d_score = (p * (d_prob - delta) * scale).astype(jnp.bfloat16)
            part = dot_nn(d_score, kr[pl.ds(j * BLK, BLK), :])
            dq = part if dq is None else dq + part
        dq_ref[rows, :] = dq.astype(jnp.bfloat16)
        st_ref[0, 0, pl.ds(n, 1), :] = col_to_row(log_total)
        st_ref[1, 0, pl.ds(n, 1), :] = col_to_row(delta)


def key_kernel(n_levels, valid_ref, k_ref, v_ref, q_ref, g_ref, st_ref, *rest):
    qf = rest[0 : 3 * n_levels : 3]
    gf = rest[1 : 3 * n_levels : 3]
    sf = rest[2 : 3 * n_levels : 3]
    dk_ref, dv_ref = rest[3 * n_levels :]
    n_cand = 1 + WIN_MAX + n_levels
    scale = HD ** (-0.5)
    causal = lax.broadcasted_iota(jnp.int32, (BLK, BLK), 0) <= lax.broadcasted_iota(
        jnp.int32, (BLK, BLK), 1
    )
    for j in range(NB):
        rows = pl.ds(j * BLK, BLK)
        kj = k_ref[rows, :]
        vj = v_ref[rows, :]
        cands = [(q_ref, g_ref, st_ref, j)]
        for o in range(1, WIN_MAX + 1):
            i = j + o
            cands.append((q_ref, g_ref, st_ref, i) if i < NB else (qf[0], gf[0], sf[0], i - NB))
        for mi in range(n_levels):
            cands.append((qf[mi], gf[mi], sf[mi], j))
        dk = None
        dv = None
        for ci, (qr, gr, sr, i) in enumerate(cands):
            qc = qr[pl.ds(i * BLK, BLK), :]
            gc = gr[pl.ds(i * BLK, BLK), :]
            lse = sr[0, 0, pl.ds(i, 1), :]
            delta = sr[1, 0, pl.ds(i, 1), :]
            s = dot_nt(kj, qc) * scale
            if ci == 0:
                s = jnp.where(causal, s, neg_large)
            else:
                s = jnp.where(valid_ref[j * n_cand + ci] != 0, s, neg_large)
            p = jnp.exp(s - lse)
            part_v = dot_nn(p.astype(jnp.bfloat16), gc)
            d_prob = dot_nt(vj, gc)
            d_score = (p * (d_prob - delta) * scale).astype(jnp.bfloat16)
            part_k = dot_nn(d_score, qc)
            dv = part_v if dv is None else dv + part_v
            dk = part_k if dk is None else dk + part_k
        dk_ref[rows, :] = dk.astype(jnp.bfloat16)
        dv_ref[rows, :] = dv.astype(jnp.bfloat16)


def head_block(part):
    return pl.BlockSpec((NB * BLK, HD), lambda h, valid: (part, h))


def stats_block(heads):
    return pl.BlockSpec((2, 1, NB, BLK), lambda h, valid: (0, h, 0, 0))


def query_call(valid, q, g, k, v, kv_from, heads, n_levels):
    tokens, features = q.shape
    in_specs = [head_block(0)] * 4
    args = [q, g, k, v]
    for kv in kv_from:
        in_specs += [head_block(0), head_block(1)]
        args += [kv, kv]
    grid_spec = pltpu.PrefetchScalarGridSpec(
        num_scalar_prefetch=1,
        grid=(heads,),
        in_specs=in_specs,
        out_specs=[head_block(0), head_block(0), stats_block(heads)],
    )
    return pl.pallas_call(
        functools.partial(query_kernel, n_levels),
        grid_spec=grid_spec,
        out_shape=[
            jax.ShapeDtypeStruct((tokens, features), jnp.bfloat16),
            jax.ShapeDtypeStruct((tokens, features), jnp.bfloat16),
            jax.ShapeDtypeStruct((2, heads, NB, BLK), jnp.float32),
        ],
        name="query_side",
    )(valid, *args)


def key_call(valid, k, v, q, g, stats, qg_from, st_from, heads, n_levels):
    tokens, features = q.shape
    in_specs = [head_block(0)] * 4 + [stats_block(heads)]
    args = [k, v, q, g, stats]
    for qg, st in zip(qg_from, st_from):
        in_specs += [head_block(0), head_block(1), stats_block(heads)]
        args += [qg, qg, st]
    grid_spec = pltpu.PrefetchScalarGridSpec(
        num_scalar_prefetch=1,
        grid=(heads,),
        in_specs=in_specs,
        out_specs=[head_block(0), head_block(0)],
    )
    return pl.pallas_call(
        functools.partial(key_kernel, n_levels),
        grid_spec=grid_spec,
        out_shape=[
            jax.ShapeDtypeStruct((tokens, features), jnp.bfloat16),
            jax.ShapeDtypeStruct((tokens, features), jnp.bfloat16),
        ],
        name="key_side",
    )(valid, *args)


def local(queries, keys, values, out_weight, d_out, window, far_select):
    tokens_local = queries.shape[0]
    heads_local = queries.shape[1] // HD
    assert tokens_local == NB * BLK
    ctx_count = lax.axis_size("ctx")
    ctx_index = lax.axis_index("ctx")
    nblocks = ctx_count * NB
    last = nblocks - 1
    levels = [m for m in range(LEVELS) if 2**m < ctx_count]
    n_levels = len(levels)
    block_ids = ctx_index * NB + jnp.arange(NB, dtype=jnp.int32)

    kv = jnp.concatenate([keys, values], axis=0)
    kv_from = [passed_along(kv, "ctx", 2**m) for m in levels]

    grad_att = lax.dot_general(
        lax.all_gather(d_out, "head", axis=1, tiled=True),
        out_weight,
        (((1,), (1,)), ((), ())),
        preferred_element_type=jnp.float32,
    )
    g = grad_att.astype(jnp.bfloat16)
    qg = jnp.concatenate([queries, g], axis=0)
    qg_from = [passed_along(qg, "ctx", -(2**m)) for m in levels]
    kv_from, qg_from = lax.optimization_barrier((kv_from, qg_from))

    own_window = lax.dynamic_slice_in_dim(window, ctx_index * NB, NB, 0)
    own_select = lax.dynamic_slice_in_dim(far_select, ctx_index * NB, NB, 0)
    valid_cols = [block_ids >= 0]
    for offset in range(1, WIN_MAX + 1):
        valid_cols.append((offset <= own_window) & (block_ids - offset >= 0))
    for m in levels:
        valid_cols.append((own_select[:, m] == 1) & (block_ids - NB * 2**m >= 0))
    valid_q = jnp.stack(valid_cols, axis=1).astype(jnp.int32).reshape(-1)

    key_cols = [block_ids >= 0]
    for offset in range(1, WIN_MAX + 1):
        qb = block_ids + offset
        key_cols.append((qb <= last) & (offset <= jnp.take(window, jnp.minimum(qb, last))))
    for m in levels:
        qb = block_ids + NB * 2**m
        key_cols.append((qb <= last) & (jnp.take(far_select[:, m], jnp.minimum(qb, last)) == 1))
    valid_k = jnp.stack(key_cols, axis=1).astype(jnp.int32).reshape(-1)

    attended, query_grad, stats = query_call(
        valid_q, queries, g, keys, values, kv_from, heads_local, n_levels
    )
    partial_out = jnp.dot(attended, out_weight, preferred_element_type=jnp.float32)
    output = lax.psum_scatter(
        partial_out.astype(jnp.bfloat16), "head", scatter_dimension=1, tiled=True
    )

    st_from = [passed_along(stats, "ctx", -(2**m)) for m in levels]
    key_grad, value_grad = key_call(
        valid_k, keys, values, queries, g, stats, qg_from, st_from, heads_local, n_levels
    )
    return output, query_grad, key_grad, value_grad


def solution(mesh):
    return jax.shard_map(
        local,
        mesh=mesh,
        in_specs=(
            P("ctx", "head"),
            P("ctx", "head"),
            P("ctx", "head"),
            P("head", None),
            P("ctx", "head"),
            P(),
            P(),
        ),
        out_specs=(P("ctx", "head"), P("ctx", "head"), P("ctx", "head"), P("ctx", "head")),
        check_vma=False,
    )
```

```python
import functools

import jax
import jax.numpy as jnp
from jax import lax
from jax.experimental import pallas as pl
from jax.experimental.pallas import tpu as pltpu
from jax.sharding import PartitionSpec as P

HD = 128
BLK = 128
WIN_MAX = 3
LEVELS = 5
NB = 4


neg_large = -1e30


def passed_along(block, axis, distance):
    devices = range(lax.axis_size(axis))
    route = [(i - distance, i) for i in devices if i - distance in devices]
    return lax.ppermute(block, axis, route)


def dot_nt(a, b):
    return lax.dot_general(a, b, (((1,), (1,)), ((), ())), preferred_element_type=jnp.float32)


def dot_nn(a, b):
    return jnp.dot(a, b, preferred_element_type=jnp.float32)


def col_to_row(col):
    eye = lax.broadcasted_iota(jnp.int32, (BLK, BLK), 0) == lax.broadcasted_iota(
        jnp.int32, (BLK, BLK), 1
    )
    return jnp.sum(jnp.where(eye, col, 0.0), axis=0, keepdims=True)


def candidate_mask(valid_ref, base, n_cand, diag):
    width = n_cand * BLK
    col = lax.broadcasted_iota(jnp.int32, (BLK, width), 1)
    allowed = (col < BLK) & diag
    for ci in range(1, n_cand):
        inside = (col >= ci * BLK) & (col < (ci + 1) * BLK)
        allowed = allowed | (inside & (valid_ref[base + ci] != 0))
    return allowed


def query_kernel(n_levels, valid_ref, q_ref, g_ref, k_ref, v_ref, *rest):
    kf = rest[0 : 2 * n_levels : 2]
    vf = rest[1 : 2 * n_levels : 2]
    att_ref, dq_ref, st_ref = rest[2 * n_levels :]
    n_cand = 1 + WIN_MAX + n_levels
    width = n_cand * BLK
    scale = HD ** (-0.5)
    col = lax.broadcasted_iota(jnp.int32, (BLK, width), 1)
    row = lax.broadcasted_iota(jnp.int32, (BLK, width), 0)
    diag = col <= row
    for n in range(NB):
        rows = pl.ds(n * BLK, BLK)
        qn = q_ref[rows, :]
        gn = g_ref[rows, :]
        cands = [(k_ref, v_ref, n)]
        for o in range(1, WIN_MAX + 1):
            j = n - o
            cands.append((k_ref, v_ref, j) if j >= 0 else (kf[0], vf[0], NB + j))
        for mi in range(n_levels):
            cands.append((kf[mi], vf[mi], n))
        kcat = jnp.concatenate([kr[pl.ds(j * BLK, BLK), :] for kr, _, j in cands], axis=0)
        vcat = jnp.concatenate([vr[pl.ds(j * BLK, BLK), :] for _, vr, j in cands], axis=0)
        allowed = candidate_mask(valid_ref, n * n_cand, n_cand, diag)
        scores = jnp.where(allowed, dot_nt(qn, kcat) * scale, neg_large)
        row_max = scores.max(axis=1, keepdims=True)
        row_total = jnp.sum(jnp.exp(scores - row_max), axis=1, keepdims=True)
        log_total = row_max + jnp.log(row_total)
        probs = jnp.exp(scores - log_total)
        att_b = dot_nn(probs.astype(jnp.bfloat16), vcat).astype(jnp.bfloat16)
        att_ref[rows, :] = att_b
        delta = jnp.sum(gn.astype(jnp.float32) * att_b.astype(jnp.float32), axis=1, keepdims=True)
        d_prob = dot_nt(gn, vcat)
        d_score = (probs * (d_prob - delta) * scale).astype(jnp.bfloat16)
        dq_ref[rows, :] = dot_nn(d_score, kcat).astype(jnp.bfloat16)
        st_ref[0, 0, pl.ds(n, 1), :] = col_to_row(log_total)
        st_ref[1, 0, pl.ds(n, 1), :] = col_to_row(delta)


def key_kernel(n_levels, valid_ref, k_ref, v_ref, q_ref, g_ref, st_ref, *rest):
    qf = rest[0 : 3 * n_levels : 3]
    gf = rest[1 : 3 * n_levels : 3]
    sf = rest[2 : 3 * n_levels : 3]
    dk_ref, dv_ref = rest[3 * n_levels :]
    n_cand = 1 + WIN_MAX + n_levels
    width = n_cand * BLK
    scale = HD ** (-0.5)
    col = lax.broadcasted_iota(jnp.int32, (BLK, width), 1)
    row = lax.broadcasted_iota(jnp.int32, (BLK, width), 0)
    diag = row <= col
    for j in range(NB):
        rows = pl.ds(j * BLK, BLK)
        kj = k_ref[rows, :]
        vj = v_ref[rows, :]
        cands = [(q_ref, g_ref, st_ref, j)]
        for o in range(1, WIN_MAX + 1):
            i = j + o
            cands.append((q_ref, g_ref, st_ref, i) if i < NB else (qf[0], gf[0], sf[0], i - NB))
        for mi in range(n_levels):
            cands.append((qf[mi], gf[mi], sf[mi], j))
        qcat = jnp.concatenate([qr[pl.ds(i * BLK, BLK), :] for qr, _, _, i in cands], axis=0)
        gcat = jnp.concatenate([gr[pl.ds(i * BLK, BLK), :] for _, gr, _, i in cands], axis=0)
        lse = jnp.concatenate([sr[0, 0, pl.ds(i, 1), :] for _, _, sr, i in cands], axis=1)
        delta = jnp.concatenate([sr[1, 0, pl.ds(i, 1), :] for _, _, sr, i in cands], axis=1)
        allowed = candidate_mask(valid_ref, j * n_cand, n_cand, diag)
        scores = jnp.where(allowed, dot_nt(kj, qcat) * scale, neg_large)
        probs = jnp.exp(scores - lse)
        dv_ref[rows, :] = dot_nn(probs.astype(jnp.bfloat16), gcat).astype(jnp.bfloat16)
        d_prob = dot_nt(vj, gcat)
        d_score = (probs * (d_prob - delta) * scale).astype(jnp.bfloat16)
        dk_ref[rows, :] = dot_nn(d_score, qcat).astype(jnp.bfloat16)


def head_block(part):
    return pl.BlockSpec((NB * BLK, HD), lambda h, valid: (part, h))


def stats_block(heads):
    return pl.BlockSpec((2, 1, NB, BLK), lambda h, valid: (0, h, 0, 0))


def query_call(valid, q, g, k, v, kv_from, heads, n_levels):
    tokens, features = q.shape
    in_specs = [head_block(0)] * 4
    args = [q, g, k, v]
    for kv in kv_from:
        in_specs += [head_block(0), head_block(1)]
        args += [kv, kv]
    grid_spec = pltpu.PrefetchScalarGridSpec(
        num_scalar_prefetch=1,
        grid=(heads,),
        in_specs=in_specs,
        out_specs=[head_block(0), head_block(0), stats_block(heads)],
    )
    return pl.pallas_call(
        functools.partial(query_kernel, n_levels),
        grid_spec=grid_spec,
        out_shape=[
            jax.ShapeDtypeStruct((tokens, features), jnp.bfloat16),
            jax.ShapeDtypeStruct((tokens, features), jnp.bfloat16),
            jax.ShapeDtypeStruct((2, heads, NB, BLK), jnp.float32),
        ],
        name="query_side",
    )(valid, *args)


def key_call(valid, k, v, q, g, stats, qg_from, st_from, heads, n_levels):
    tokens, features = q.shape
    in_specs = [head_block(0)] * 4 + [stats_block(heads)]
    args = [k, v, q, g, stats]
    for qg, st in zip(qg_from, st_from):
        in_specs += [head_block(0), head_block(1), stats_block(heads)]
        args += [qg, qg, st]
    grid_spec = pltpu.PrefetchScalarGridSpec(
        num_scalar_prefetch=1,
        grid=(heads,),
        in_specs=in_specs,
        out_specs=[head_block(0), head_block(0)],
    )
    return pl.pallas_call(
        functools.partial(key_kernel, n_levels),
        grid_spec=grid_spec,
        out_shape=[
            jax.ShapeDtypeStruct((tokens, features), jnp.bfloat16),
            jax.ShapeDtypeStruct((tokens, features), jnp.bfloat16),
        ],
        name="key_side",
    )(valid, *args)


def local(queries, keys, values, out_weight, d_out, window, far_select):
    tokens_local = queries.shape[0]
    heads_local = queries.shape[1] // HD
    assert tokens_local == NB * BLK
    ctx_count = lax.axis_size("ctx")
    ctx_index = lax.axis_index("ctx")
    nblocks = ctx_count * NB
    last = nblocks - 1
    levels = [m for m in range(LEVELS) if 2**m < ctx_count]
    n_levels = len(levels)
    block_ids = ctx_index * NB + jnp.arange(NB, dtype=jnp.int32)

    kv = jnp.concatenate([keys, values], axis=0)
    kv_from = [passed_along(kv, "ctx", 2**m) for m in levels]

    grad_att = lax.dot_general(
        lax.all_gather(d_out, "head", axis=1, tiled=True),
        out_weight,
        (((1,), (1,)), ((), ())),
        preferred_element_type=jnp.float32,
    )
    g = grad_att.astype(jnp.bfloat16)
    qg = jnp.concatenate([queries, g], axis=0)
    qg_from = [passed_along(qg, "ctx", -(2**m)) for m in levels]
    kv_from, qg_from = lax.optimization_barrier((kv_from, qg_from))

    own_window = lax.dynamic_slice_in_dim(window, ctx_index * NB, NB, 0)
    own_select = lax.dynamic_slice_in_dim(far_select, ctx_index * NB, NB, 0)
    valid_cols = [block_ids >= 0]
    for offset in range(1, WIN_MAX + 1):
        valid_cols.append((offset <= own_window) & (block_ids - offset >= 0))
    for m in levels:
        valid_cols.append((own_select[:, m] == 1) & (block_ids - NB * 2**m >= 0))
    valid_q = jnp.stack(valid_cols, axis=1).astype(jnp.int32).reshape(-1)

    key_cols = [block_ids >= 0]
    for offset in range(1, WIN_MAX + 1):
        qb = block_ids + offset
        key_cols.append((qb <= last) & (offset <= jnp.take(window, jnp.minimum(qb, last))))
    for m in levels:
        qb = block_ids + NB * 2**m
        key_cols.append((qb <= last) & (jnp.take(far_select[:, m], jnp.minimum(qb, last)) == 1))
    valid_k = jnp.stack(key_cols, axis=1).astype(jnp.int32).reshape(-1)

    attended, query_grad, stats = query_call(
        valid_q, queries, g, keys, values, kv_from, heads_local, n_levels
    )
    partial_out = jnp.dot(attended, out_weight, preferred_element_type=jnp.float32)
    output = lax.psum_scatter(
        partial_out.astype(jnp.bfloat16), "head", scatter_dimension=1, tiled=True
    )

    st_from = [passed_along(stats, "ctx", -(2**m)) for m in levels]
    key_grad, value_grad = key_call(
        valid_k, keys, values, queries, g, stats, qg_from, st_from, heads_local, n_levels
    )
    return output, query_grad, key_grad, value_grad


def solution(mesh):
    return jax.shard_map(
        local,
        mesh=mesh,
        in_specs=(
            P("ctx", "head"),
            P("ctx", "head"),
            P("ctx", "head"),
            P("head", None),
            P("ctx", "head"),
            P(),
            P(),
        ),
        out_specs=(P("ctx", "head"), P("ctx", "head"), P("ctx", "head"), P("ctx", "head")),
        check_vma=False,
    )
```

```python
import functools

import jax
import jax.numpy as jnp
from jax import lax
from jax.experimental import pallas as pl
from jax.experimental.pallas import tpu as pltpu
from jax.sharding import PartitionSpec as P

HD = 128
BLK = 128
WIN_MAX = 3
LEVELS = 5
NB = 4


neg_large = -1e30


def passed_along(block, axis, distance):
    devices = range(lax.axis_size(axis))
    route = [(i - distance, i) for i in devices if i - distance in devices]
    return lax.ppermute(block, axis, route)


def dot_nt(a, b):
    return lax.dot_general(a, b, (((1,), (1,)), ((), ())), preferred_element_type=jnp.float32)


def dot_nn(a, b):
    return jnp.dot(a, b, preferred_element_type=jnp.float32)


def col_to_row(col):
    eye = lax.broadcasted_iota(jnp.int32, (BLK, BLK), 0) == lax.broadcasted_iota(
        jnp.int32, (BLK, BLK), 1
    )
    return jnp.sum(jnp.where(eye, col, 0.0), axis=0, keepdims=True)


def candidate_mask(valid_ref, base, n_cand, diag):
    width = n_cand * BLK
    col = lax.broadcasted_iota(jnp.int32, (BLK, width), 1)
    allowed = (col < BLK) & diag
    for ci in range(1, n_cand):
        inside = (col >= ci * BLK) & (col < (ci + 1) * BLK)
        allowed = allowed | (inside & (valid_ref[base + ci] != 0))
    return allowed


def query_kernel(n_levels, valid_ref, q_ref, g_ref, k_ref, v_ref, *rest):
    kf = rest[0 : 2 * n_levels : 2]
    vf = rest[1 : 2 * n_levels : 2]
    att_ref, dq_ref, st_ref = rest[2 * n_levels :]
    n_cand = 1 + WIN_MAX + n_levels
    width = n_cand * BLK
    scale = HD ** (-0.5)
    col = lax.broadcasted_iota(jnp.int32, (BLK, width), 1)
    row = lax.broadcasted_iota(jnp.int32, (BLK, width), 0)
    diag = col <= row
    for n in range(NB):
        rows = pl.ds(n * BLK, BLK)
        qn = q_ref[rows, :]
        gn = g_ref[rows, :]
        cands = [(k_ref, v_ref, n)]
        for o in range(1, WIN_MAX + 1):
            j = n - o
            cands.append((k_ref, v_ref, j) if j >= 0 else (kf[0], vf[0], NB + j))
        for mi in range(n_levels):
            cands.append((kf[mi], vf[mi], n))
        kcat = jnp.concatenate([kr[pl.ds(j * BLK, BLK), :] for kr, _, j in cands], axis=0)
        vcat = jnp.concatenate([vr[pl.ds(j * BLK, BLK), :] for _, vr, j in cands], axis=0)
        allowed = candidate_mask(valid_ref, n * n_cand, n_cand, diag)
        scores = jnp.where(allowed, dot_nt(qn, kcat) * scale, neg_large)
        row_max = scores.max(axis=1, keepdims=True)
        row_total = jnp.sum(jnp.exp(scores - row_max), axis=1, keepdims=True)
        log_total = row_max + jnp.log(row_total)
        probs = jnp.exp(scores - log_total)
        att_b = dot_nn(probs.astype(jnp.bfloat16), vcat).astype(jnp.bfloat16)
        att_ref[rows, :] = att_b
        delta = jnp.sum(gn.astype(jnp.float32) * att_b.astype(jnp.float32), axis=1, keepdims=True)
        d_prob = dot_nt(gn, vcat)
        d_score = (probs * (d_prob - delta) * scale).astype(jnp.bfloat16)
        dq_ref[rows, :] = dot_nn(d_score, kcat).astype(jnp.bfloat16)
        st_ref[0, 0, pl.ds(n, 1), :] = col_to_row(log_total)
        st_ref[1, 0, pl.ds(n, 1), :] = col_to_row(delta)


def key_kernel(n_levels, valid_ref, k_ref, v_ref, q_ref, g_ref, st_ref, *rest):
    qf = rest[0 : 3 * n_levels : 3]
    gf = rest[1 : 3 * n_levels : 3]
    sf = rest[2 : 3 * n_levels : 3]
    dk_ref, dv_ref = rest[3 * n_levels :]
    n_cand = 1 + WIN_MAX + n_levels
    width = n_cand * BLK
    scale = HD ** (-0.5)
    col = lax.broadcasted_iota(jnp.int32, (BLK, width), 1)
    row = lax.broadcasted_iota(jnp.int32, (BLK, width), 0)
    diag = row <= col
    for j in range(NB):
        rows = pl.ds(j * BLK, BLK)
        kj = k_ref[rows, :]
        vj = v_ref[rows, :]
        cands = [(q_ref, g_ref, st_ref, j)]
        for o in range(1, WIN_MAX + 1):
            i = j + o
            cands.append((q_ref, g_ref, st_ref, i) if i < NB else (qf[0], gf[0], sf[0], i - NB))
        for mi in range(n_levels):
            cands.append((qf[mi], gf[mi], sf[mi], j))
        qcat = jnp.concatenate([qr[pl.ds(i * BLK, BLK), :] for qr, _, _, i in cands], axis=0)
        gcat = jnp.concatenate([gr[pl.ds(i * BLK, BLK), :] for _, gr, _, i in cands], axis=0)
        lse = jnp.concatenate([sr[0, 0, pl.ds(i, 1), :] for _, _, sr, i in cands], axis=1)
        delta = jnp.concatenate([sr[1, 0, pl.ds(i, 1), :] for _, _, sr, i in cands], axis=1)
        allowed = candidate_mask(valid_ref, j * n_cand, n_cand, diag)
        scores = jnp.where(allowed, dot_nt(kj, qcat) * scale, neg_large)
        probs = jnp.exp(scores - lse)
        dv_ref[rows, :] = dot_nn(probs.astype(jnp.bfloat16), gcat).astype(jnp.bfloat16)
        d_prob = dot_nt(vj, gcat)
        d_score = (probs * (d_prob - delta) * scale).astype(jnp.bfloat16)
        dk_ref[rows, :] = dot_nn(d_score, qcat).astype(jnp.bfloat16)


def head_block(part):
    return pl.BlockSpec((NB * BLK, HD), lambda h, valid: (part, h))


def stats_block(heads):
    return pl.BlockSpec((2, 1, NB, BLK), lambda h, valid: (0, h, 0, 0))


def query_call(valid, q, g, k, v, kv_from, heads, n_levels):
    tokens, features = q.shape
    in_specs = [head_block(0)] * 4
    args = [q, g, k, v]
    for kv in kv_from:
        in_specs += [head_block(0), head_block(1)]
        args += [kv, kv]
    grid_spec = pltpu.PrefetchScalarGridSpec(
        num_scalar_prefetch=1,
        grid=(heads,),
        in_specs=in_specs,
        out_specs=[head_block(0), head_block(0), stats_block(heads)],
    )
    return pl.pallas_call(
        functools.partial(query_kernel, n_levels),
        grid_spec=grid_spec,
        out_shape=[
            jax.ShapeDtypeStruct((tokens, features), jnp.bfloat16),
            jax.ShapeDtypeStruct((tokens, features), jnp.bfloat16),
            jax.ShapeDtypeStruct((2, heads, NB, BLK), jnp.float32),
        ],
        name="query_side",
    )(valid, *args)


def key_call(valid, k, v, q, g, stats, q_from, g_from, st_from, heads, n_levels):
    tokens, features = q.shape
    in_specs = [head_block(0)] * 4 + [stats_block(heads)]
    args = [k, v, q, g, stats]
    for qa, ga, st in zip(q_from, g_from, st_from):
        in_specs += [head_block(0), head_block(0), stats_block(heads)]
        args += [qa, ga, st]
    grid_spec = pltpu.PrefetchScalarGridSpec(
        num_scalar_prefetch=1,
        grid=(heads,),
        in_specs=in_specs,
        out_specs=[head_block(0), head_block(0)],
    )
    return pl.pallas_call(
        functools.partial(key_kernel, n_levels),
        grid_spec=grid_spec,
        out_shape=[
            jax.ShapeDtypeStruct((tokens, features), jnp.bfloat16),
            jax.ShapeDtypeStruct((tokens, features), jnp.bfloat16),
        ],
        name="key_side",
    )(valid, *args)


def local(queries, keys, values, out_weight, d_out, window, far_select):
    tokens_local = queries.shape[0]
    heads_local = queries.shape[1] // HD
    assert tokens_local == NB * BLK
    ctx_count = lax.axis_size("ctx")
    ctx_index = lax.axis_index("ctx")
    nblocks = ctx_count * NB
    last = nblocks - 1
    levels = [m for m in range(LEVELS) if 2**m < ctx_count]
    n_levels = len(levels)
    block_ids = ctx_index * NB + jnp.arange(NB, dtype=jnp.int32)

    own_window = lax.dynamic_slice_in_dim(window, ctx_index * NB, NB, 0)
    own_select = lax.dynamic_slice_in_dim(far_select, ctx_index * NB, NB, 0)
    valid_cols = [block_ids >= 0]
    for offset in range(1, WIN_MAX + 1):
        valid_cols.append((offset <= own_window) & (block_ids - offset >= 0))
    for m in levels:
        valid_cols.append((own_select[:, m] == 1) & (block_ids - NB * 2**m >= 0))
    valid_q = jnp.stack(valid_cols, axis=1).astype(jnp.int32).reshape(-1)

    key_cols = [block_ids >= 0]
    for offset in range(1, WIN_MAX + 1):
        qb = block_ids + offset
        key_cols.append((qb <= last) & (offset <= jnp.take(window, jnp.minimum(qb, last))))
    for m in levels:
        qb = block_ids + NB * 2**m
        key_cols.append((qb <= last) & (jnp.take(far_select[:, m], jnp.minimum(qb, last)) == 1))
    valid_k = jnp.stack(key_cols, axis=1).astype(jnp.int32).reshape(-1)

    kv = jnp.concatenate([keys, values], axis=0)
    kv_from = [passed_along(kv, "ctx", 2**m) for m in levels]
    q_from = [passed_along(queries, "ctx", -(2**m)) for m in levels]

    grad_att = lax.dot_general(
        lax.all_gather(d_out, "head", axis=1, tiled=True),
        out_weight,
        (((1,), (1,)), ((), ())),
        preferred_element_type=jnp.float32,
    )
    g = grad_att.astype(jnp.bfloat16)
    g_from = [passed_along(g, "ctx", -(2**m)) for m in levels]
    kv_from, q_from, g_from, valid_q, valid_k = lax.optimization_barrier(
        (kv_from, q_from, g_from, valid_q, valid_k)
    )

    attended, query_grad, stats = query_call(
        valid_q, queries, g, keys, values, kv_from, heads_local, n_levels
    )
    partial_out = jnp.dot(attended, out_weight, preferred_element_type=jnp.float32)
    output = lax.psum_scatter(
        partial_out.astype(jnp.bfloat16), "head", scatter_dimension=1, tiled=True
    )

    st_from = [passed_along(stats, "ctx", -(2**m)) for m in levels]
    key_grad, value_grad = key_call(
        valid_k, keys, values, queries, g, stats, q_from, g_from, st_from, heads_local, n_levels
    )
    return output, query_grad, key_grad, value_grad


def solution(mesh):
    return jax.shard_map(
        local,
        mesh=mesh,
        in_specs=(
            P("ctx", "head"),
            P("ctx", "head"),
            P("ctx", "head"),
            P("head", None),
            P("ctx", "head"),
            P(),
            P(),
        ),
        out_specs=(P("ctx", "head"), P("ctx", "head"), P("ctx", "head"), P("ctx", "head")),
        check_vma=False,
    )
```

```python
import functools

import jax
import jax.numpy as jnp
from jax import lax
from jax.experimental import pallas as pl
from jax.experimental.pallas import tpu as pltpu
from jax.sharding import PartitionSpec as P

HD = 128
BLK = 128
WIN_MAX = 3
LEVELS = 5
NB = 4


neg_large = -1e30


def passed_along(block, axis, distance):
    devices = range(lax.axis_size(axis))
    route = [(i - distance, i) for i in devices if i - distance in devices]
    return lax.ppermute(block, axis, route)


def dot_nt(a, b):
    return lax.dot_general(a, b, (((1,), (1,)), ((), ())), preferred_element_type=jnp.float32)


def dot_nn(a, b):
    return jnp.dot(a, b, preferred_element_type=jnp.float32)


def col_to_row(col):
    eye = lax.broadcasted_iota(jnp.int32, (BLK, BLK), 0) == lax.broadcasted_iota(
        jnp.int32, (BLK, BLK), 1
    )
    return jnp.sum(jnp.where(eye, col, 0.0), axis=0, keepdims=True)


def candidate_mask(valid_ref, base, n_cand, diag):
    width = n_cand * BLK
    col = lax.broadcasted_iota(jnp.int32, (BLK, width), 1)
    allowed = (col < BLK) & diag
    for ci in range(1, n_cand):
        inside = (col >= ci * BLK) & (col < (ci + 1) * BLK)
        allowed = allowed | (inside & (valid_ref[base + ci] != 0))
    return allowed


def query_kernel(n_levels, valid_ref, q_ref, g_ref, k_ref, v_ref, *rest):
    kf = rest[0 : 2 * n_levels : 2]
    vf = rest[1 : 2 * n_levels : 2]
    att_ref, dq_ref, st_ref = rest[2 * n_levels :]
    n_cand = 1 + WIN_MAX + n_levels
    width = n_cand * BLK
    scale = HD ** (-0.5)
    col = lax.broadcasted_iota(jnp.int32, (BLK, width), 1)
    row = lax.broadcasted_iota(jnp.int32, (BLK, width), 0)
    diag = col <= row
    for n in range(NB):
        rows = pl.ds(n * BLK, BLK)
        qn = q_ref[rows, :]
        gn = g_ref[rows, :]
        cands = [(k_ref, v_ref, n)]
        for o in range(1, WIN_MAX + 1):
            j = n - o
            cands.append((k_ref, v_ref, j) if j >= 0 else (kf[0], vf[0], NB + j))
        for mi in range(n_levels):
            cands.append((kf[mi], vf[mi], n))
        kcat = jnp.concatenate([kr[pl.ds(j * BLK, BLK), :] for kr, _, j in cands], axis=0)
        vcat = jnp.concatenate([vr[pl.ds(j * BLK, BLK), :] for _, vr, j in cands], axis=0)
        allowed = candidate_mask(valid_ref, n * n_cand, n_cand, diag)
        scores = jnp.where(allowed, dot_nt(qn, kcat) * scale, neg_large)
        row_max = scores.max(axis=1, keepdims=True)
        row_total = jnp.sum(jnp.exp(scores - row_max), axis=1, keepdims=True)
        log_total = row_max + jnp.log(row_total)
        probs = jnp.exp(scores - log_total)
        att_b = dot_nn(probs.astype(jnp.bfloat16), vcat).astype(jnp.bfloat16)
        att_ref[rows, :] = att_b
        delta = jnp.sum(gn.astype(jnp.float32) * att_b.astype(jnp.float32), axis=1, keepdims=True)
        d_prob = dot_nt(gn, vcat)
        d_score = (probs * (d_prob - delta) * scale).astype(jnp.bfloat16)
        dq_ref[rows, :] = dot_nn(d_score, kcat).astype(jnp.bfloat16)
        st_ref[0, 0, pl.ds(n, 1), :] = col_to_row(log_total)
        st_ref[1, 0, pl.ds(n, 1), :] = col_to_row(delta)


def key_kernel(n_levels, valid_ref, k_ref, v_ref, q_ref, g_ref, st_ref, *rest):
    qf = rest[0 : 3 * n_levels : 3]
    gf = rest[1 : 3 * n_levels : 3]
    sf = rest[2 : 3 * n_levels : 3]
    dk_ref, dv_ref = rest[3 * n_levels :]
    n_cand = 1 + WIN_MAX + n_levels
    width = n_cand * BLK
    scale = HD ** (-0.5)
    col = lax.broadcasted_iota(jnp.int32, (BLK, width), 1)
    row = lax.broadcasted_iota(jnp.int32, (BLK, width), 0)
    diag = row <= col
    for j in range(NB):
        rows = pl.ds(j * BLK, BLK)
        kj = k_ref[rows, :]
        vj = v_ref[rows, :]
        cands = [(q_ref, g_ref, st_ref, j)]
        for o in range(1, WIN_MAX + 1):
            i = j + o
            cands.append((q_ref, g_ref, st_ref, i) if i < NB else (qf[0], gf[0], sf[0], i - NB))
        for mi in range(n_levels):
            cands.append((qf[mi], gf[mi], sf[mi], j))
        qcat = jnp.concatenate([qr[pl.ds(i * BLK, BLK), :] for qr, _, _, i in cands], axis=0)
        gcat = jnp.concatenate([gr[pl.ds(i * BLK, BLK), :] for _, gr, _, i in cands], axis=0)
        lse = jnp.concatenate([sr[0, 0, pl.ds(i, 1), :] for _, _, sr, i in cands], axis=1)
        delta = jnp.concatenate([sr[1, 0, pl.ds(i, 1), :] for _, _, sr, i in cands], axis=1)
        allowed = candidate_mask(valid_ref, j * n_cand, n_cand, diag)
        scores = jnp.where(allowed, dot_nt(kj, qcat) * scale, neg_large)
        probs = jnp.exp(scores - lse)
        dv_ref[rows, :] = dot_nn(probs.astype(jnp.bfloat16), gcat).astype(jnp.bfloat16)
        d_prob = dot_nt(vj, gcat)
        d_score = (probs * (d_prob - delta) * scale).astype(jnp.bfloat16)
        dk_ref[rows, :] = dot_nn(d_score, qcat).astype(jnp.bfloat16)


def head_block(part):
    return pl.BlockSpec((NB * BLK, HD), lambda h, valid: (part, h))


def stats_block(heads):
    return pl.BlockSpec((2, 1, NB, BLK), lambda h, valid: (0, h, 0, 0))


def query_call(valid, q, g, k, v, kv_from, heads, n_levels):
    tokens, features = q.shape
    in_specs = [head_block(0)] * 4
    args = [q, g, k, v]
    for kv in kv_from:
        in_specs += [head_block(0), head_block(1)]
        args += [kv, kv]
    grid_spec = pltpu.PrefetchScalarGridSpec(
        num_scalar_prefetch=1,
        grid=(heads,),
        in_specs=in_specs,
        out_specs=[head_block(0), head_block(0), stats_block(heads)],
    )
    return pl.pallas_call(
        functools.partial(query_kernel, n_levels),
        grid_spec=grid_spec,
        out_shape=[
            jax.ShapeDtypeStruct((tokens, features), jnp.bfloat16),
            jax.ShapeDtypeStruct((tokens, features), jnp.bfloat16),
            jax.ShapeDtypeStruct((2, heads, NB, BLK), jnp.float32),
        ],
        name="query_side",
    )(valid, *args)


def key_call(valid, k, v, q, g, stats, q_from, g_from, st_from, heads, n_levels):
    tokens, features = q.shape
    in_specs = [head_block(0)] * 4 + [stats_block(heads)]
    args = [k, v, q, g, stats]
    for qa, ga, st in zip(q_from, g_from, st_from):
        in_specs += [head_block(0), head_block(0), stats_block(heads)]
        args += [qa, ga, st]
    grid_spec = pltpu.PrefetchScalarGridSpec(
        num_scalar_prefetch=1,
        grid=(heads,),
        in_specs=in_specs,
        out_specs=[head_block(0), head_block(0)],
    )
    return pl.pallas_call(
        functools.partial(key_kernel, n_levels),
        grid_spec=grid_spec,
        out_shape=[
            jax.ShapeDtypeStruct((tokens, features), jnp.bfloat16),
            jax.ShapeDtypeStruct((tokens, features), jnp.bfloat16),
        ],
        name="key_side",
    )(valid, *args)


def local(queries, keys, values, out_weight, d_out, window, far_select):
    tokens_local = queries.shape[0]
    heads_local = queries.shape[1] // HD
    assert tokens_local == NB * BLK
    ctx_count = lax.axis_size("ctx")
    ctx_index = lax.axis_index("ctx")
    nblocks = ctx_count * NB
    last = nblocks - 1
    levels = [m for m in range(LEVELS) if 2**m < ctx_count]
    n_levels = len(levels)
    block_ids = ctx_index * NB + jnp.arange(NB, dtype=jnp.int32)

    own_window = lax.dynamic_slice_in_dim(window, ctx_index * NB, NB, 0)
    own_select = lax.dynamic_slice_in_dim(far_select, ctx_index * NB, NB, 0)
    valid_cols = [block_ids >= 0]
    for offset in range(1, WIN_MAX + 1):
        valid_cols.append((offset <= own_window) & (block_ids - offset >= 0))
    for m in levels:
        valid_cols.append((own_select[:, m] == 1) & (block_ids - NB * 2**m >= 0))
    valid_q = jnp.stack(valid_cols, axis=1).astype(jnp.int32).reshape(-1)

    key_cols = [block_ids >= 0]
    for offset in range(1, WIN_MAX + 1):
        qb = block_ids + offset
        key_cols.append((qb <= last) & (offset <= jnp.take(window, jnp.minimum(qb, last))))
    for m in levels:
        qb = block_ids + NB * 2**m
        key_cols.append((qb <= last) & (jnp.take(far_select[:, m], jnp.minimum(qb, last)) == 1))
    valid_k = jnp.stack(key_cols, axis=1).astype(jnp.int32).reshape(-1)

    kv = jnp.concatenate([keys, values], axis=0)
    kv_from = [passed_along(kv, "ctx", 2**m) for m in levels]
    q_from = [passed_along(queries, "ctx", -(2**m)) for m in levels]

    grad_att = lax.dot_general(
        lax.all_gather(d_out, "head", axis=1, tiled=True),
        out_weight,
        (((1,), (1,)), ((), ())),
        preferred_element_type=jnp.float32,
    )
    g = grad_att.astype(jnp.bfloat16)
    g_from = [passed_along(g, "ctx", -(2**m)) for m in levels]
    weight_cols = lax.all_to_all(out_weight, "head", 1, 0, tiled=True)
    kv_from, q_from, g_from, valid_q, valid_k, weight_cols = lax.optimization_barrier(
        (kv_from, q_from, g_from, valid_q, valid_k, weight_cols)
    )

    attended, query_grad, stats = query_call(
        valid_q, queries, g, keys, values, kv_from, heads_local, n_levels
    )
    output = jnp.dot(
        lax.all_gather(attended, "head", axis=1, tiled=True),
        weight_cols,
        preferred_element_type=jnp.float32,
    ).astype(jnp.bfloat16)

    st_from = [passed_along(stats, "ctx", -(2**m)) for m in levels]
    key_grad, value_grad = key_call(
        valid_k, keys, values, queries, g, stats, q_from, g_from, st_from, heads_local, n_levels
    )
    return output, query_grad, key_grad, value_grad


def solution(mesh):
    return jax.shard_map(
        local,
        mesh=mesh,
        in_specs=(
            P("ctx", "head"),
            P("ctx", "head"),
            P("ctx", "head"),
            P("head", None),
            P("ctx", "head"),
            P(),
            P(),
        ),
        out_specs=(P("ctx", "head"), P("ctx", "head"), P("ctx", "head"), P("ctx", "head")),
        check_vma=False,
    )
```

```python
import functools

import jax
import jax.numpy as jnp
from jax import lax
from jax.experimental import pallas as pl
from jax.experimental.pallas import tpu as pltpu
from jax.sharding import PartitionSpec as P

HD = 128
BLK = 128
WIN_MAX = 3
LEVELS = 5
NB = 4


neg_large = -1e30


def passed_along(block, axis, distance):
    devices = range(lax.axis_size(axis))
    route = [(i - distance, i) for i in devices if i - distance in devices]
    return lax.ppermute(block, axis, route)


def dot_nt(a, b):
    return lax.dot_general(a, b, (((1,), (1,)), ((), ())), preferred_element_type=jnp.float32)


def dot_nn(a, b):
    return jnp.dot(a, b, preferred_element_type=jnp.float32)


def col_to_row(col):
    eye = lax.broadcasted_iota(jnp.int32, (BLK, BLK), 0) == lax.broadcasted_iota(
        jnp.int32, (BLK, BLK), 1
    )
    return jnp.sum(jnp.where(eye, col, 0.0), axis=0, keepdims=True)


def candidate_mask(valid_ref, base, n_cand, diag):
    width = n_cand * BLK
    col = lax.broadcasted_iota(jnp.int32, (BLK, width), 1)
    allowed = (col < BLK) & diag
    for ci in range(1, n_cand):
        inside = (col >= ci * BLK) & (col < (ci + 1) * BLK)
        allowed = allowed | (inside & (valid_ref[base + ci] != 0))
    return allowed


def row_to_col(row):
    eye = lax.broadcasted_iota(jnp.int32, (BLK, BLK), 0) == lax.broadcasted_iota(
        jnp.int32, (BLK, BLK), 1
    )
    return jnp.sum(jnp.where(eye, row, 0.0), axis=1, keepdims=True)


def query_blocks(n_levels, valid_ref, q_ref, k_ref, v_ref, kv_refs):
    kf = kv_refs[0::2]
    vf = kv_refs[1::2]
    n_cand = 1 + WIN_MAX + n_levels
    scale = HD ** (-0.5)
    col = lax.broadcasted_iota(jnp.int32, (BLK, n_cand * BLK), 1)
    row = lax.broadcasted_iota(jnp.int32, (BLK, n_cand * BLK), 0)
    diag = col <= row
    for n in range(NB):
        rows = pl.ds(n * BLK, BLK)
        qn = q_ref[rows, :]
        cands = [(k_ref, v_ref, n)]
        for o in range(1, WIN_MAX + 1):
            j = n - o
            cands.append((k_ref, v_ref, j) if j >= 0 else (kf[0], vf[0], NB + j))
        for mi in range(n_levels):
            cands.append((kf[mi], vf[mi], n))
        kcat = jnp.concatenate([kr[pl.ds(j * BLK, BLK), :] for kr, _, j in cands], axis=0)
        vcat = jnp.concatenate([vr[pl.ds(j * BLK, BLK), :] for _, vr, j in cands], axis=0)
        allowed = candidate_mask(valid_ref, n * n_cand, n_cand, diag)
        scores = jnp.where(allowed, dot_nt(qn, kcat) * scale, neg_large)
        yield n, rows, kcat, vcat, scores


def query_fwd_kernel(n_levels, valid_ref, q_ref, g_ref, k_ref, v_ref, *rest):
    att_ref, st_ref = rest[2 * n_levels :]
    blocks = query_blocks(n_levels, valid_ref, q_ref, k_ref, v_ref, rest[: 2 * n_levels])
    for n, rows, kcat, vcat, scores in blocks:
        row_max = scores.max(axis=1, keepdims=True)
        row_total = jnp.sum(jnp.exp(scores - row_max), axis=1, keepdims=True)
        log_total = row_max + jnp.log(row_total)
        probs = jnp.exp(scores - log_total)
        att_b = dot_nn(probs.astype(jnp.bfloat16), vcat).astype(jnp.bfloat16)
        att_ref[rows, :] = att_b
        gn = g_ref[rows, :]
        delta = jnp.sum(gn.astype(jnp.float32) * att_b.astype(jnp.float32), axis=1, keepdims=True)
        st_ref[0, 0, pl.ds(n, 1), :] = col_to_row(log_total)
        st_ref[1, 0, pl.ds(n, 1), :] = col_to_row(delta)


def query_bwd_kernel(n_levels, valid_ref, q_ref, g_ref, k_ref, v_ref, st_ref, *rest):
    dq_ref = rest[2 * n_levels]
    scale = HD ** (-0.5)
    blocks = query_blocks(n_levels, valid_ref, q_ref, k_ref, v_ref, rest[: 2 * n_levels])
    for n, rows, kcat, vcat, scores in blocks:
        log_total = row_to_col(st_ref[0, 0, pl.ds(n, 1), :])
        delta = row_to_col(st_ref[1, 0, pl.ds(n, 1), :])
        probs = jnp.exp(scores - log_total)
        d_prob = dot_nt(g_ref[rows, :], vcat)
        d_score = (probs * (d_prob - delta) * scale).astype(jnp.bfloat16)
        dq_ref[rows, :] = dot_nn(d_score, kcat).astype(jnp.bfloat16)


def key_kernel(n_levels, valid_ref, k_ref, v_ref, q_ref, g_ref, st_ref, *rest):
    qf = rest[0 : 3 * n_levels : 3]
    gf = rest[1 : 3 * n_levels : 3]
    sf = rest[2 : 3 * n_levels : 3]
    dk_ref, dv_ref = rest[3 * n_levels :]
    n_cand = 1 + WIN_MAX + n_levels
    width = n_cand * BLK
    scale = HD ** (-0.5)
    col = lax.broadcasted_iota(jnp.int32, (BLK, width), 1)
    row = lax.broadcasted_iota(jnp.int32, (BLK, width), 0)
    diag = row <= col
    for j in range(NB):
        rows = pl.ds(j * BLK, BLK)
        kj = k_ref[rows, :]
        vj = v_ref[rows, :]
        cands = [(q_ref, g_ref, st_ref, j)]
        for o in range(1, WIN_MAX + 1):
            i = j + o
            cands.append((q_ref, g_ref, st_ref, i) if i < NB else (qf[0], gf[0], sf[0], i - NB))
        for mi in range(n_levels):
            cands.append((qf[mi], gf[mi], sf[mi], j))
        qcat = jnp.concatenate([qr[pl.ds(i * BLK, BLK), :] for qr, _, _, i in cands], axis=0)
        gcat = jnp.concatenate([gr[pl.ds(i * BLK, BLK), :] for _, gr, _, i in cands], axis=0)
        lse = jnp.concatenate([sr[0, 0, pl.ds(i, 1), :] for _, _, sr, i in cands], axis=1)
        delta = jnp.concatenate([sr[1, 0, pl.ds(i, 1), :] for _, _, sr, i in cands], axis=1)
        allowed = candidate_mask(valid_ref, j * n_cand, n_cand, diag)
        scores = jnp.where(allowed, dot_nt(kj, qcat) * scale, neg_large)
        probs = jnp.exp(scores - lse)
        dv_ref[rows, :] = dot_nn(probs.astype(jnp.bfloat16), gcat).astype(jnp.bfloat16)
        d_prob = dot_nt(vj, gcat)
        d_score = (probs * (d_prob - delta) * scale).astype(jnp.bfloat16)
        dk_ref[rows, :] = dot_nn(d_score, qcat).astype(jnp.bfloat16)


def head_block(part):
    return pl.BlockSpec((NB * BLK, HD), lambda h, valid: (part, h))


def stats_block(heads):
    return pl.BlockSpec((2, 1, NB, BLK), lambda h, valid: (0, h, 0, 0))


def query_call(kernel, valid, q, g, k, v, kv_from, extra, heads, n_levels, out_specs, out_shape, name):
    in_specs = [head_block(0)] * 4 + [stats_block(heads)] * len(extra)
    args = [q, g, k, v] + list(extra)
    for kv in kv_from:
        in_specs += [head_block(0), head_block(1)]
        args += [kv, kv]
    grid_spec = pltpu.PrefetchScalarGridSpec(
        num_scalar_prefetch=1,
        grid=(heads,),
        in_specs=in_specs,
        out_specs=out_specs,
    )
    return pl.pallas_call(
        functools.partial(kernel, n_levels),
        grid_spec=grid_spec,
        out_shape=out_shape,
        name=name,
    )(valid, *args)


def key_call(valid, k, v, q, g, stats, q_from, g_from, st_from, heads, n_levels):
    tokens, features = q.shape
    in_specs = [head_block(0)] * 4 + [stats_block(heads)]
    args = [k, v, q, g, stats]
    for qa, ga, st in zip(q_from, g_from, st_from):
        in_specs += [head_block(0), head_block(0), stats_block(heads)]
        args += [qa, ga, st]
    grid_spec = pltpu.PrefetchScalarGridSpec(
        num_scalar_prefetch=1,
        grid=(heads,),
        in_specs=in_specs,
        out_specs=[head_block(0), head_block(0)],
    )
    return pl.pallas_call(
        functools.partial(key_kernel, n_levels),
        grid_spec=grid_spec,
        out_shape=[
            jax.ShapeDtypeStruct((tokens, features), jnp.bfloat16),
            jax.ShapeDtypeStruct((tokens, features), jnp.bfloat16),
        ],
        name="key_side",
    )(valid, *args)


def local(queries, keys, values, out_weight, d_out, window, far_select):
    tokens_local = queries.shape[0]
    heads_local = queries.shape[1] // HD
    assert tokens_local == NB * BLK
    ctx_count = lax.axis_size("ctx")
    ctx_index = lax.axis_index("ctx")
    nblocks = ctx_count * NB
    last = nblocks - 1
    levels = [m for m in range(LEVELS) if 2**m < ctx_count]
    n_levels = len(levels)
    block_ids = ctx_index * NB + jnp.arange(NB, dtype=jnp.int32)

    own_window = lax.dynamic_slice_in_dim(window, ctx_index * NB, NB, 0)
    own_select = lax.dynamic_slice_in_dim(far_select, ctx_index * NB, NB, 0)
    valid_cols = [block_ids >= 0]
    for offset in range(1, WIN_MAX + 1):
        valid_cols.append((offset <= own_window) & (block_ids - offset >= 0))
    for m in levels:
        valid_cols.append((own_select[:, m] == 1) & (block_ids - NB * 2**m >= 0))
    valid_q = jnp.stack(valid_cols, axis=1).astype(jnp.int32).reshape(-1)

    key_cols = [block_ids >= 0]
    for offset in range(1, WIN_MAX + 1):
        qb = block_ids + offset
        key_cols.append((qb <= last) & (offset <= jnp.take(window, jnp.minimum(qb, last))))
    for m in levels:
        qb = block_ids + NB * 2**m
        key_cols.append((qb <= last) & (jnp.take(far_select[:, m], jnp.minimum(qb, last)) == 1))
    valid_k = jnp.stack(key_cols, axis=1).astype(jnp.int32).reshape(-1)

    kv = jnp.concatenate([keys, values], axis=0)
    kv_from = [passed_along(kv, "ctx", 2**m) for m in levels]
    q_from = [passed_along(queries, "ctx", -(2**m)) for m in levels]

    grad_att = lax.dot_general(
        lax.all_gather(d_out, "head", axis=1, tiled=True),
        out_weight,
        (((1,), (1,)), ((), ())),
        preferred_element_type=jnp.float32,
    )
    g = grad_att.astype(jnp.bfloat16)
    g_from = [passed_along(g, "ctx", -(2**m)) for m in levels]
    weight_cols = lax.all_to_all(out_weight, "head", 1, 0, tiled=True)
    kv_from, q_from, g_from, valid_q, valid_k, weight_cols = lax.optimization_barrier(
        (kv_from, q_from, g_from, valid_q, valid_k, weight_cols)
    )

    flat = jax.ShapeDtypeStruct(queries.shape, jnp.bfloat16)
    stats_shape = jax.ShapeDtypeStruct((2, heads_local, NB, BLK), jnp.float32)
    attended, stats = query_call(
        query_fwd_kernel, valid_q, queries, g, keys, values, kv_from, [], heads_local, n_levels,
        [head_block(0), stats_block(heads_local)], [flat, stats_shape], "query_forward",
    )
    (query_grad,) = query_call(
        query_bwd_kernel, valid_q, queries, g, keys, values, kv_from, [stats], heads_local,
        n_levels, [head_block(0)], [flat], "query_backward",
    )
    output = jnp.dot(
        lax.all_gather(attended, "head", axis=1, tiled=True),
        weight_cols,
        preferred_element_type=jnp.float32,
    ).astype(jnp.bfloat16)

    st_from = [passed_along(stats, "ctx", -(2**m)) for m in levels]
    key_grad, value_grad = key_call(
        valid_k, keys, values, queries, g, stats, q_from, g_from, st_from, heads_local, n_levels
    )
    return output, query_grad, key_grad, value_grad


def solution(mesh):
    return jax.shard_map(
        local,
        mesh=mesh,
        in_specs=(
            P("ctx", "head"),
            P("ctx", "head"),
            P("ctx", "head"),
            P("head", None),
            P("ctx", "head"),
            P(),
            P(),
        ),
        out_specs=(P("ctx", "head"), P("ctx", "head"), P("ctx", "head"), P("ctx", "head")),
        check_vma=False,
    )
```

```python
import functools

import jax
import jax.numpy as jnp
from jax import lax
from jax.experimental import pallas as pl
from jax.experimental.pallas import tpu as pltpu
from jax.sharding import PartitionSpec as P

HD = 128
BLK = 128
WIN_MAX = 3
LEVELS = 5
NB = 4


neg_large = -1e30


def passed_along(block, axis, distance):
    devices = range(lax.axis_size(axis))
    route = [(i - distance, i) for i in devices if i - distance in devices]
    return lax.ppermute(block, axis, route)


def dot_nt(a, b):
    return lax.dot_general(a, b, (((1,), (1,)), ((), ())), preferred_element_type=jnp.float32)


def dot_nn(a, b):
    return jnp.dot(a, b, preferred_element_type=jnp.float32)


def col_to_row(col):
    eye = lax.broadcasted_iota(jnp.int32, (BLK, BLK), 0) == lax.broadcasted_iota(
        jnp.int32, (BLK, BLK), 1
    )
    return jnp.sum(jnp.where(eye, col, 0.0), axis=0, keepdims=True)


SLOTS = 3


def candidate_mask(oks, diag):
    width = (1 + len(oks)) * BLK
    col = lax.broadcasted_iota(jnp.int32, (BLK, width), 1)
    allowed = (col < BLK) & diag[:, :width]
    for ci, ok in enumerate(oks, start=1):
        inside = (col >= ci * BLK) & (col < (ci + 1) * BLK)
        allowed = allowed | (inside & ok)
    return allowed


def compacted(valid_ref, base, n_cand):
    oks, ranks = [], []
    count = jnp.int32(0)
    for ci in range(1, n_cand):
        ok = valid_ref[base + ci] != 0
        oks.append(ok)
        ranks.append(count)
        count = count + ok.astype(jnp.int32)
    return oks, ranks, count


def pick(blocks, oks, ranks, slot):
    out = jnp.zeros_like(blocks[0])
    for block, ok, rank in zip(blocks, oks, ranks):
        out = jnp.where(ok & (rank == slot), block, out)
    return out


def narrow_or_full(valid_ref, base, n_cand, body):
    oks, ranks, count = compacted(valid_ref, base, n_cand)

    @pl.when(count <= SLOTS)
    def _():
        body(lambda blocks: [pick(blocks, oks, ranks, p) for p in range(SLOTS)],
             [count > p for p in range(SLOTS)])

    @pl.when(count > SLOTS)
    def _():
        body(lambda blocks: blocks, oks)


def query_kernel(n_levels, valid_ref, q_ref, g_ref, k_ref, v_ref, *rest):
    kf = rest[0 : 2 * n_levels : 2]
    vf = rest[1 : 2 * n_levels : 2]
    att_ref, dq_ref, st_ref = rest[2 * n_levels :]
    n_cand = 1 + WIN_MAX + n_levels
    width = n_cand * BLK
    scale = HD ** (-0.5)
    col = lax.broadcasted_iota(jnp.int32, (BLK, width), 1)
    row = lax.broadcasted_iota(jnp.int32, (BLK, width), 0)
    diag = col <= row
    for n in range(NB):
        rows = pl.ds(n * BLK, BLK)
        cands = [(k_ref, v_ref, n)]
        for o in range(1, WIN_MAX + 1):
            j = n - o
            cands.append((k_ref, v_ref, j) if j >= 0 else (kf[0], vf[0], NB + j))
        for mi in range(n_levels):
            cands.append((kf[mi], vf[mi], n))

        def body(select, oks, rows=rows, cands=cands, n=n):
            qn = q_ref[rows, :]
            gn = g_ref[rows, :]
            ks = [kr[pl.ds(j * BLK, BLK), :] for kr, _, j in cands]
            vs = [vr[pl.ds(j * BLK, BLK), :] for _, vr, j in cands]
            kcat = jnp.concatenate([ks[0]] + select(ks[1:]), axis=0)
            vcat = jnp.concatenate([vs[0]] + select(vs[1:]), axis=0)
            allowed = candidate_mask(oks, diag)
            scores = jnp.where(allowed, dot_nt(qn, kcat) * scale, neg_large)
            row_max = scores.max(axis=1, keepdims=True)
            row_total = jnp.sum(jnp.exp(scores - row_max), axis=1, keepdims=True)
            log_total = row_max + jnp.log(row_total)
            probs = jnp.exp(scores - log_total)
            att_b = dot_nn(probs.astype(jnp.bfloat16), vcat).astype(jnp.bfloat16)
            att_ref[rows, :] = att_b
            delta = jnp.sum(gn.astype(jnp.float32) * att_b.astype(jnp.float32), axis=1, keepdims=True)
            d_prob = dot_nt(gn, vcat)
            d_score = (probs * (d_prob - delta) * scale).astype(jnp.bfloat16)
            dq_ref[rows, :] = dot_nn(d_score, kcat).astype(jnp.bfloat16)
            st_ref[0, 0, pl.ds(n, 1), :] = col_to_row(log_total)
            st_ref[1, 0, pl.ds(n, 1), :] = col_to_row(delta)

        narrow_or_full(valid_ref, n * n_cand, n_cand, body)


def key_kernel(n_levels, valid_ref, k_ref, v_ref, q_ref, g_ref, st_ref, *rest):
    qf = rest[0 : 3 * n_levels : 3]
    gf = rest[1 : 3 * n_levels : 3]
    sf = rest[2 : 3 * n_levels : 3]
    dk_ref, dv_ref = rest[3 * n_levels :]
    n_cand = 1 + WIN_MAX + n_levels
    width = n_cand * BLK
    scale = HD ** (-0.5)
    col = lax.broadcasted_iota(jnp.int32, (BLK, width), 1)
    row = lax.broadcasted_iota(jnp.int32, (BLK, width), 0)
    diag = row <= col
    for j in range(NB):
        rows = pl.ds(j * BLK, BLK)
        cands = [(q_ref, g_ref, st_ref, j)]
        for o in range(1, WIN_MAX + 1):
            i = j + o
            cands.append((q_ref, g_ref, st_ref, i) if i < NB else (qf[0], gf[0], sf[0], i - NB))
        for mi in range(n_levels):
            cands.append((qf[mi], gf[mi], sf[mi], j))

        def body(select, oks, rows=rows, cands=cands):
            kj = k_ref[rows, :]
            vj = v_ref[rows, :]
            qs = [qr[pl.ds(i * BLK, BLK), :] for qr, _, _, i in cands]
            gs = [gr[pl.ds(i * BLK, BLK), :] for _, gr, _, i in cands]
            ls = [sr[0, 0, pl.ds(i, 1), :] for _, _, sr, i in cands]
            ds = [sr[1, 0, pl.ds(i, 1), :] for _, _, sr, i in cands]
            qcat = jnp.concatenate([qs[0]] + select(qs[1:]), axis=0)
            gcat = jnp.concatenate([gs[0]] + select(gs[1:]), axis=0)
            lse = jnp.concatenate([ls[0]] + select(ls[1:]), axis=1)
            delta = jnp.concatenate([ds[0]] + select(ds[1:]), axis=1)
            allowed = candidate_mask(oks, diag)
            scores = jnp.where(allowed, dot_nt(kj, qcat) * scale, neg_large)
            probs = jnp.exp(scores - lse)
            dv_ref[rows, :] = dot_nn(probs.astype(jnp.bfloat16), gcat).astype(jnp.bfloat16)
            d_prob = dot_nt(vj, gcat)
            d_score = (probs * (d_prob - delta) * scale).astype(jnp.bfloat16)
            dk_ref[rows, :] = dot_nn(d_score, qcat).astype(jnp.bfloat16)

        narrow_or_full(valid_ref, j * n_cand, n_cand, body)


def head_block(part):
    return pl.BlockSpec((NB * BLK, HD), lambda h, valid: (part, h))


def stats_block(heads):
    return pl.BlockSpec((2, 1, NB, BLK), lambda h, valid: (0, h, 0, 0))


def query_call(valid, q, g, k, v, kv_from, heads, n_levels):
    tokens, features = q.shape
    in_specs = [head_block(0)] * 4
    args = [q, g, k, v]
    for kv in kv_from:
        in_specs += [head_block(0), head_block(1)]
        args += [kv, kv]
    grid_spec = pltpu.PrefetchScalarGridSpec(
        num_scalar_prefetch=1,
        grid=(heads,),
        in_specs=in_specs,
        out_specs=[head_block(0), head_block(0), stats_block(heads)],
    )
    return pl.pallas_call(
        functools.partial(query_kernel, n_levels),
        grid_spec=grid_spec,
        out_shape=[
            jax.ShapeDtypeStruct((tokens, features), jnp.bfloat16),
            jax.ShapeDtypeStruct((tokens, features), jnp.bfloat16),
            jax.ShapeDtypeStruct((2, heads, NB, BLK), jnp.float32),
        ],
        name="query_side",
    )(valid, *args)


def key_call(valid, k, v, q, g, stats, q_from, g_from, st_from, heads, n_levels):
    tokens, features = q.shape
    in_specs = [head_block(0)] * 4 + [stats_block(heads)]
    args = [k, v, q, g, stats]
    for qa, ga, st in zip(q_from, g_from, st_from):
        in_specs += [head_block(0), head_block(0), stats_block(heads)]
        args += [qa, ga, st]
    grid_spec = pltpu.PrefetchScalarGridSpec(
        num_scalar_prefetch=1,
        grid=(heads,),
        in_specs=in_specs,
        out_specs=[head_block(0), head_block(0)],
    )
    return pl.pallas_call(
        functools.partial(key_kernel, n_levels),
        grid_spec=grid_spec,
        out_shape=[
            jax.ShapeDtypeStruct((tokens, features), jnp.bfloat16),
            jax.ShapeDtypeStruct((tokens, features), jnp.bfloat16),
        ],
        name="key_side",
    )(valid, *args)


def local(queries, keys, values, out_weight, d_out, window, far_select):
    tokens_local = queries.shape[0]
    heads_local = queries.shape[1] // HD
    assert tokens_local == NB * BLK
    ctx_count = lax.axis_size("ctx")
    ctx_index = lax.axis_index("ctx")
    nblocks = ctx_count * NB
    last = nblocks - 1
    levels = [m for m in range(LEVELS) if 2**m < ctx_count]
    n_levels = len(levels)
    block_ids = ctx_index * NB + jnp.arange(NB, dtype=jnp.int32)

    own_window = lax.dynamic_slice_in_dim(window, ctx_index * NB, NB, 0)
    own_select = lax.dynamic_slice_in_dim(far_select, ctx_index * NB, NB, 0)
    valid_cols = [block_ids >= 0]
    for offset in range(1, WIN_MAX + 1):
        valid_cols.append((offset <= own_window) & (block_ids - offset >= 0))
    for m in levels:
        valid_cols.append((own_select[:, m] == 1) & (block_ids - NB * 2**m >= 0))
    valid_q = jnp.stack(valid_cols, axis=1).astype(jnp.int32).reshape(-1)

    key_cols = [block_ids >= 0]
    for offset in range(1, WIN_MAX + 1):
        qb = block_ids + offset
        key_cols.append((qb <= last) & (offset <= jnp.take(window, jnp.minimum(qb, last))))
    for m in levels:
        qb = block_ids + NB * 2**m
        key_cols.append((qb <= last) & (jnp.take(far_select[:, m], jnp.minimum(qb, last)) == 1))
    valid_k = jnp.stack(key_cols, axis=1).astype(jnp.int32).reshape(-1)

    kv = jnp.concatenate([keys, values], axis=0)
    kv_from = [passed_along(kv, "ctx", 2**m) for m in levels]
    q_from = [passed_along(queries, "ctx", -(2**m)) for m in levels]

    grad_att = lax.dot_general(
        lax.all_gather(d_out, "head", axis=1, tiled=True),
        out_weight,
        (((1,), (1,)), ((), ())),
        preferred_element_type=jnp.float32,
    )
    g = grad_att.astype(jnp.bfloat16)
    g_from = [passed_along(g, "ctx", -(2**m)) for m in levels]
    weight_cols = lax.all_to_all(out_weight, "head", 1, 0, tiled=True)
    kv_from, q_from, g_from, valid_q, valid_k, weight_cols = lax.optimization_barrier(
        (kv_from, q_from, g_from, valid_q, valid_k, weight_cols)
    )

    attended, query_grad, stats = query_call(
        valid_q, queries, g, keys, values, kv_from, heads_local, n_levels
    )
    output = jnp.dot(
        lax.all_gather(attended, "head", axis=1, tiled=True),
        weight_cols,
        preferred_element_type=jnp.float32,
    ).astype(jnp.bfloat16)

    st_from = [passed_along(stats, "ctx", -(2**m)) for m in levels]
    key_grad, value_grad = key_call(
        valid_k, keys, values, queries, g, stats, q_from, g_from, st_from, heads_local, n_levels
    )
    return output, query_grad, key_grad, value_grad


def solution(mesh):
    return jax.shard_map(
        local,
        mesh=mesh,
        in_specs=(
            P("ctx", "head"),
            P("ctx", "head"),
            P("ctx", "head"),
            P("head", None),
            P("ctx", "head"),
            P(),
            P(),
        ),
        out_specs=(P("ctx", "head"), P("ctx", "head"), P("ctx", "head"), P("ctx", "head")),
        check_vma=False,
    )
```

```python
import functools

import jax
import jax.numpy as jnp
from jax import lax
from jax.experimental import pallas as pl
from jax.experimental.pallas import tpu as pltpu
from jax.sharding import PartitionSpec as P

HD = 128
BLK = 128
WIN_MAX = 3
LEVELS = 5
NB = 4


neg_large = -1e30


def passed_along(block, axis, distance):
    devices = range(lax.axis_size(axis))
    route = [(i - distance, i) for i in devices if i - distance in devices]
    return lax.ppermute(block, axis, route)


def dot_nt(a, b):
    return lax.dot_general(a, b, (((1,), (1,)), ((), ())), preferred_element_type=jnp.float32)


def dot_nn(a, b):
    return jnp.dot(a, b, preferred_element_type=jnp.float32)


def col_to_row(col):
    eye = lax.broadcasted_iota(jnp.int32, (BLK, BLK), 0) == lax.broadcasted_iota(
        jnp.int32, (BLK, BLK), 1
    )
    return jnp.sum(jnp.where(eye, col, 0.0), axis=0, keepdims=True)


def candidate_mask(valid_ref, base, n_cand, diag):
    width = n_cand * BLK
    col = lax.broadcasted_iota(jnp.int32, (BLK, width), 1)
    allowed = (col < BLK) & diag
    for ci in range(1, n_cand):
        inside = (col >= ci * BLK) & (col < (ci + 1) * BLK)
        allowed = allowed | (inside & (valid_ref[base + ci] != 0))
    return allowed


def query_kernel(n_levels, valid_ref, q_ref, g_ref, k_ref, v_ref, *rest):
    kf = rest[0 : 2 * n_levels : 2]
    vf = rest[1 : 2 * n_levels : 2]
    att_ref, dq_ref, st_ref = rest[2 * n_levels :]
    n_cand = 1 + WIN_MAX + n_levels
    width = n_cand * BLK
    scale = HD ** (-0.5)
    col = lax.broadcasted_iota(jnp.int32, (BLK, width), 1)
    row = lax.broadcasted_iota(jnp.int32, (BLK, width), 0)
    diag = col <= row
    for n in range(NB):
        rows = pl.ds(n * BLK, BLK)
        qn = q_ref[rows, :]
        gn = g_ref[rows, :]
        cands = [(k_ref, v_ref, n)]
        for o in range(1, WIN_MAX + 1):
            j = n - o
            cands.append((k_ref, v_ref, j) if j >= 0 else (kf[0], vf[0], NB + j))
        for mi in range(n_levels):
            cands.append((kf[mi], vf[mi], n))
        kcat = jnp.concatenate([kr[pl.ds(j * BLK, BLK), :] for kr, _, j in cands], axis=0)
        vcat = jnp.concatenate([vr[pl.ds(j * BLK, BLK), :] for _, vr, j in cands], axis=0)
        allowed = candidate_mask(valid_ref, n * n_cand, n_cand, diag)
        scores = jnp.where(allowed, dot_nt(qn, kcat) * scale, neg_large)
        row_max = scores.max(axis=1, keepdims=True)
        row_total = jnp.sum(jnp.exp(scores - row_max), axis=1, keepdims=True)
        log_total = row_max + jnp.log(row_total)
        probs = jnp.exp(scores - log_total)
        att_b = dot_nn(probs.astype(jnp.bfloat16), vcat).astype(jnp.bfloat16)
        att_ref[rows, :] = att_b
        delta = jnp.sum(gn.astype(jnp.float32) * att_b.astype(jnp.float32), axis=1, keepdims=True)
        d_prob = dot_nt(gn, vcat)
        d_score = (probs * (d_prob - delta) * scale).astype(jnp.bfloat16)
        dq_ref[rows, :] = dot_nn(d_score, kcat).astype(jnp.bfloat16)
        st_ref[0, 0, pl.ds(n, 1), :] = col_to_row(log_total)
        st_ref[1, 0, pl.ds(n, 1), :] = col_to_row(delta)


def key_kernel(n_levels, valid_ref, k_ref, v_ref, q_ref, g_ref, st_ref, *rest):
    qf = rest[0 : 3 * n_levels : 3]
    gf = rest[1 : 3 * n_levels : 3]
    sf = rest[2 : 3 * n_levels : 3]
    dk_ref, dv_ref = rest[3 * n_levels :]
    n_cand = 1 + WIN_MAX + n_levels
    width = n_cand * BLK
    scale = HD ** (-0.5)
    col = lax.broadcasted_iota(jnp.int32, (BLK, width), 1)
    row = lax.broadcasted_iota(jnp.int32, (BLK, width), 0)
    diag = row <= col
    for j in range(NB):
        rows = pl.ds(j * BLK, BLK)
        kj = k_ref[rows, :]
        vj = v_ref[rows, :]
        cands = [(q_ref, g_ref, st_ref, j)]
        for o in range(1, WIN_MAX + 1):
            i = j + o
            cands.append((q_ref, g_ref, st_ref, i) if i < NB else (qf[0], gf[0], sf[0], i - NB))
        for mi in range(n_levels):
            cands.append((qf[mi], gf[mi], sf[mi], j))
        qcat = jnp.concatenate([qr[pl.ds(i * BLK, BLK), :] for qr, _, _, i in cands], axis=0)
        gcat = jnp.concatenate([gr[pl.ds(i * BLK, BLK), :] for _, gr, _, i in cands], axis=0)
        lse = jnp.concatenate([sr[0, 0, pl.ds(i, 1), :] for _, _, sr, i in cands], axis=1)
        delta = jnp.concatenate([sr[1, 0, pl.ds(i, 1), :] for _, _, sr, i in cands], axis=1)
        allowed = candidate_mask(valid_ref, j * n_cand, n_cand, diag)
        scores = jnp.where(allowed, dot_nt(kj, qcat) * scale, neg_large)
        probs = jnp.exp(scores - lse)
        dv_ref[rows, :] = dot_nn(probs.astype(jnp.bfloat16), gcat).astype(jnp.bfloat16)
        d_prob = dot_nt(vj, gcat)
        d_score = (probs * (d_prob - delta) * scale).astype(jnp.bfloat16)
        dk_ref[rows, :] = dot_nn(d_score, qcat).astype(jnp.bfloat16)


def head_block(part):
    return pl.BlockSpec((NB * BLK, HD), lambda h, valid: (part, h))


def stats_block(heads):
    return pl.BlockSpec((2, 1, NB, BLK), lambda h, valid: (0, h, 0, 0))


def query_call(valid, q, g, k, v, kv_from, heads, n_levels):
    tokens, features = q.shape
    in_specs = [head_block(0)] * 4
    args = [q, g, k, v]
    for kv in kv_from:
        in_specs += [head_block(0), head_block(1)]
        args += [kv, kv]
    grid_spec = pltpu.PrefetchScalarGridSpec(
        num_scalar_prefetch=1,
        grid=(heads,),
        in_specs=in_specs,
        out_specs=[head_block(0), head_block(0), stats_block(heads)],
    )
    return pl.pallas_call(
        functools.partial(query_kernel, n_levels),
        grid_spec=grid_spec,
        out_shape=[
            jax.ShapeDtypeStruct((tokens, features), jnp.bfloat16),
            jax.ShapeDtypeStruct((tokens, features), jnp.bfloat16),
            jax.ShapeDtypeStruct((2, heads, NB, BLK), jnp.float32),
        ],
        name="query_side",
    )(valid, *args)


def key_call(valid, k, v, q, g, stats, q_from, g_from, st_from, heads, n_levels):
    tokens, features = q.shape
    in_specs = [head_block(0)] * 4 + [stats_block(heads)]
    args = [k, v, q, g, stats]
    for qa, ga, st in zip(q_from, g_from, st_from):
        in_specs += [head_block(0), head_block(0), stats_block(heads)]
        args += [qa, ga, st]
    grid_spec = pltpu.PrefetchScalarGridSpec(
        num_scalar_prefetch=1,
        grid=(heads,),
        in_specs=in_specs,
        out_specs=[head_block(0), head_block(0)],
    )
    return pl.pallas_call(
        functools.partial(key_kernel, n_levels),
        grid_spec=grid_spec,
        out_shape=[
            jax.ShapeDtypeStruct((tokens, features), jnp.bfloat16),
            jax.ShapeDtypeStruct((tokens, features), jnp.bfloat16),
        ],
        name="key_side",
    )(valid, *args)


def local(queries, keys, values, out_weight, d_out, window, far_select):
    tokens_local = queries.shape[0]
    heads_local = queries.shape[1] // HD
    assert tokens_local == NB * BLK
    ctx_count = lax.axis_size("ctx")
    ctx_index = lax.axis_index("ctx")
    nblocks = ctx_count * NB
    last = nblocks - 1
    levels = [m for m in range(LEVELS) if 2**m < ctx_count]
    n_levels = len(levels)
    block_ids = ctx_index * NB + jnp.arange(NB, dtype=jnp.int32)

    own_window = lax.dynamic_slice_in_dim(window, ctx_index * NB, NB, 0)
    own_select = lax.dynamic_slice_in_dim(far_select, ctx_index * NB, NB, 0)
    valid_cols = [block_ids >= 0]
    for offset in range(1, WIN_MAX + 1):
        valid_cols.append((offset <= own_window) & (block_ids - offset >= 0))
    for m in levels:
        valid_cols.append((own_select[:, m] == 1) & (block_ids - NB * 2**m >= 0))
    valid_q = jnp.stack(valid_cols, axis=1).astype(jnp.int32).reshape(-1)

    key_cols = [block_ids >= 0]
    for offset in range(1, WIN_MAX + 1):
        qb = block_ids + offset
        key_cols.append((qb <= last) & (offset <= jnp.take(window, jnp.minimum(qb, last))))
    for m in levels:
        qb = block_ids + NB * 2**m
        key_cols.append((qb <= last) & (jnp.take(far_select[:, m], jnp.minimum(qb, last)) == 1))
    valid_k = jnp.stack(key_cols, axis=1).astype(jnp.int32).reshape(-1)

    kv = jnp.concatenate([keys, values], axis=0)
    kv_from = [passed_along(kv, "ctx", 2**m) for m in levels]
    q_near = passed_along(queries, "ctx", -1)

    grad_att = lax.dot_general(
        lax.all_gather(d_out, "head", axis=1, tiled=True),
        out_weight,
        (((1,), (1,)), ((), ())),
        preferred_element_type=jnp.float32,
    )
    g = grad_att.astype(jnp.bfloat16)
    g_near = passed_along(g, "ctx", -1)
    qg = jnp.concatenate([queries, g], axis=0)
    qg_far = [passed_along(qg, "ctx", -(2**m)) for m in levels[1:]]
    q_from = [q_near] + [pair[: queries.shape[0]] for pair in qg_far]
    g_from = [g_near] + [pair[queries.shape[0] :] for pair in qg_far]
    weight_cols = lax.all_to_all(out_weight, "head", 1, 0, tiled=True)
    kv_from, q_from, g_from, valid_q, valid_k, weight_cols = lax.optimization_barrier(
        (kv_from, q_from, g_from, valid_q, valid_k, weight_cols)
    )

    attended, query_grad, stats = query_call(
        valid_q, queries, g, keys, values, kv_from, heads_local, n_levels
    )
    output = jnp.dot(
        lax.all_gather(attended, "head", axis=1, tiled=True),
        weight_cols,
        preferred_element_type=jnp.float32,
    ).astype(jnp.bfloat16)

    st_from = [passed_along(stats, "ctx", -(2**m)) for m in levels]
    key_grad, value_grad = key_call(
        valid_k, keys, values, queries, g, stats, q_from, g_from, st_from, heads_local, n_levels
    )
    return output, query_grad, key_grad, value_grad


def solution(mesh):
    return jax.shard_map(
        local,
        mesh=mesh,
        in_specs=(
            P("ctx", "head"),
            P("ctx", "head"),
            P("ctx", "head"),
            P("head", None),
            P("ctx", "head"),
            P(),
            P(),
        ),
        out_specs=(P("ctx", "head"), P("ctx", "head"), P("ctx", "head"), P("ctx", "head")),
        check_vma=False,
    )
```

```python
import functools

import jax
import jax.numpy as jnp
from jax import lax
from jax.experimental import pallas as pl
from jax.experimental.pallas import tpu as pltpu
from jax.sharding import PartitionSpec as P

HD = 128
BLK = 128
WIN_MAX = 3
LEVELS = 5
NB = 4


neg_large = -1e30


def passed_along(block, axis, distance):
    devices = range(lax.axis_size(axis))
    route = [(i - distance, i) for i in devices if i - distance in devices]
    return lax.ppermute(block, axis, route)


def dot_nt(a, b):
    return lax.dot_general(a, b, (((1,), (1,)), ((), ())), preferred_element_type=jnp.float32)


def dot_nn(a, b):
    return jnp.dot(a, b, preferred_element_type=jnp.float32)


def col_to_row(col):
    eye = lax.broadcasted_iota(jnp.int32, (BLK, BLK), 0) == lax.broadcasted_iota(
        jnp.int32, (BLK, BLK), 1
    )
    return jnp.sum(jnp.where(eye, col, 0.0), axis=0, keepdims=True)


def candidate_mask(valid_ref, base, n_cand, diag):
    width = n_cand * BLK
    col = lax.broadcasted_iota(jnp.int32, (BLK, width), 1)
    allowed = (col < BLK) & diag
    for ci in range(1, n_cand):
        inside = (col >= ci * BLK) & (col < (ci + 1) * BLK)
        allowed = allowed | (inside & (valid_ref[base + ci] != 0))
    return allowed


def query_kernel(n_levels, valid_ref, q_ref, g_ref, k_ref, v_ref, *rest):
    kf = rest[0 : 2 * n_levels : 2]
    vf = rest[1 : 2 * n_levels : 2]
    att_ref, dq_ref, st_ref = rest[2 * n_levels :]
    n_cand = 1 + WIN_MAX + n_levels
    width = n_cand * BLK
    scale = HD ** (-0.5)
    col = lax.broadcasted_iota(jnp.int32, (BLK, width), 1)
    row = lax.broadcasted_iota(jnp.int32, (BLK, width), 0)
    diag = col <= row
    for n in range(NB):
        rows = pl.ds(n * BLK, BLK)
        qn = q_ref[rows, :]
        gn = g_ref[rows, :]
        cands = [(k_ref, v_ref, n)]
        for o in range(1, WIN_MAX + 1):
            j = n - o
            cands.append((k_ref, v_ref, j) if j >= 0 else (kf[0], vf[0], NB + j))
        for mi in range(n_levels):
            cands.append((kf[mi], vf[mi], n))
        kcat = jnp.concatenate([kr[pl.ds(j * BLK, BLK), :] for kr, _, j in cands], axis=0)
        vcat = jnp.concatenate([vr[pl.ds(j * BLK, BLK), :] for _, vr, j in cands], axis=0)
        allowed = candidate_mask(valid_ref, n * n_cand, n_cand, diag)
        scores = jnp.where(allowed, dot_nt(qn, kcat) * scale, neg_large)
        row_max = scores.max(axis=1, keepdims=True)
        row_total = jnp.sum(jnp.exp(scores - row_max), axis=1, keepdims=True)
        log_total = row_max + jnp.log(row_total)
        probs = jnp.exp(scores - log_total)
        att_b = dot_nn(probs.astype(jnp.bfloat16), vcat).astype(jnp.bfloat16)
        att_ref[rows, :] = att_b
        delta = jnp.sum(gn.astype(jnp.float32) * att_b.astype(jnp.float32), axis=1, keepdims=True)
        d_prob = dot_nt(gn, vcat)
        d_score = (probs * (d_prob - delta) * scale).astype(jnp.bfloat16)
        dq_ref[rows, :] = dot_nn(d_score, kcat).astype(jnp.bfloat16)
        st_ref[0, 0, pl.ds(n, 1), :] = col_to_row(log_total)
        st_ref[1, 0, pl.ds(n, 1), :] = col_to_row(delta)


def key_kernel(n_levels, valid_ref, k_ref, v_ref, q_ref, g_ref, st_ref, *rest):
    qf = rest[0 : 3 * n_levels : 3]
    gf = rest[1 : 3 * n_levels : 3]
    sf = rest[2 : 3 * n_levels : 3]
    dk_ref, dv_ref = rest[3 * n_levels :]
    n_cand = 1 + WIN_MAX + n_levels
    width = n_cand * BLK
    scale = HD ** (-0.5)
    col = lax.broadcasted_iota(jnp.int32, (BLK, width), 1)
    row = lax.broadcasted_iota(jnp.int32, (BLK, width), 0)
    diag = row <= col
    for j in range(NB):
        rows = pl.ds(j * BLK, BLK)
        kj = k_ref[rows, :]
        vj = v_ref[rows, :]
        cands = [(q_ref, g_ref, st_ref, j)]
        for o in range(1, WIN_MAX + 1):
            i = j + o
            cands.append((q_ref, g_ref, st_ref, i) if i < NB else (qf[0], gf[0], sf[0], i - NB))
        for mi in range(n_levels):
            cands.append((qf[mi], gf[mi], sf[mi], j))
        qcat = jnp.concatenate([qr[pl.ds(i * BLK, BLK), :] for qr, _, _, i in cands], axis=0)
        gcat = jnp.concatenate([gr[pl.ds(i * BLK, BLK), :] for _, gr, _, i in cands], axis=0)
        lse = jnp.concatenate([sr[0, 0, pl.ds(i, 1), :] for _, _, sr, i in cands], axis=1)
        delta = jnp.concatenate([sr[1, 0, pl.ds(i, 1), :] for _, _, sr, i in cands], axis=1)
        allowed = candidate_mask(valid_ref, j * n_cand, n_cand, diag)
        scores = jnp.where(allowed, dot_nt(kj, qcat) * scale, neg_large)
        probs = jnp.exp(scores - lse)
        dv_ref[rows, :] = dot_nn(probs.astype(jnp.bfloat16), gcat).astype(jnp.bfloat16)
        d_prob = dot_nt(vj, gcat)
        d_score = (probs * (d_prob - delta) * scale).astype(jnp.bfloat16)
        dk_ref[rows, :] = dot_nn(d_score, qcat).astype(jnp.bfloat16)


def head_block(part):
    return pl.BlockSpec((NB * BLK, HD), lambda h, valid: (part, h))


def stats_block(heads):
    return pl.BlockSpec((2, 1, NB, BLK), lambda h, valid: (0, h, 0, 0))


def query_call(valid, q, g, k, v, kv_from, heads, n_levels):
    tokens, features = q.shape
    in_specs = [head_block(0)] * 4
    args = [q, g, k, v]
    for kv in kv_from:
        in_specs += [head_block(0), head_block(1)]
        args += [kv, kv]
    grid_spec = pltpu.PrefetchScalarGridSpec(
        num_scalar_prefetch=1,
        grid=(heads,),
        in_specs=in_specs,
        out_specs=[head_block(0), head_block(0), stats_block(heads)],
    )
    return pl.pallas_call(
        functools.partial(query_kernel, n_levels),
        grid_spec=grid_spec,
        out_shape=[
            jax.ShapeDtypeStruct((tokens, features), jnp.bfloat16),
            jax.ShapeDtypeStruct((tokens, features), jnp.bfloat16),
            jax.ShapeDtypeStruct((2, heads, NB, BLK), jnp.float32),
        ],
        name="query_side",
    )(valid, *args)


def key_call(valid, k, v, q, g, stats, q_from, g_from, st_from, heads, n_levels):
    tokens, features = q.shape
    in_specs = [head_block(0)] * 4 + [stats_block(heads)]
    args = [k, v, q, g, stats]
    for qa, ga, st in zip(q_from, g_from, st_from):
        in_specs += [head_block(0), head_block(0), stats_block(heads)]
        args += [qa, ga, st]
    grid_spec = pltpu.PrefetchScalarGridSpec(
        num_scalar_prefetch=1,
        grid=(heads,),
        in_specs=in_specs,
        out_specs=[head_block(0), head_block(0)],
    )
    return pl.pallas_call(
        functools.partial(key_kernel, n_levels),
        grid_spec=grid_spec,
        out_shape=[
            jax.ShapeDtypeStruct((tokens, features), jnp.bfloat16),
            jax.ShapeDtypeStruct((tokens, features), jnp.bfloat16),
        ],
        name="key_side",
    )(valid, *args)


def local(queries, keys, values, out_weight, d_out, window, far_select):
    tokens_local = queries.shape[0]
    heads_local = queries.shape[1] // HD
    assert tokens_local == NB * BLK
    ctx_count = lax.axis_size("ctx")
    ctx_index = lax.axis_index("ctx")
    nblocks = ctx_count * NB
    last = nblocks - 1
    levels = [m for m in range(LEVELS) if 2**m < ctx_count]
    n_levels = len(levels)
    block_ids = ctx_index * NB + jnp.arange(NB, dtype=jnp.int32)

    own_window = lax.dynamic_slice_in_dim(window, ctx_index * NB, NB, 0)
    own_select = lax.dynamic_slice_in_dim(far_select, ctx_index * NB, NB, 0)
    valid_cols = [block_ids >= 0]
    for offset in range(1, WIN_MAX + 1):
        valid_cols.append((offset <= own_window) & (block_ids - offset >= 0))
    for m in levels:
        valid_cols.append((own_select[:, m] == 1) & (block_ids - NB * 2**m >= 0))
    valid_q = jnp.stack(valid_cols, axis=1).astype(jnp.int32).reshape(-1)

    key_cols = [block_ids >= 0]
    for offset in range(1, WIN_MAX + 1):
        qb = block_ids + offset
        key_cols.append((qb <= last) & (offset <= jnp.take(window, jnp.minimum(qb, last))))
    for m in levels:
        qb = block_ids + NB * 2**m
        key_cols.append((qb <= last) & (jnp.take(far_select[:, m], jnp.minimum(qb, last)) == 1))
    valid_k = jnp.stack(key_cols, axis=1).astype(jnp.int32).reshape(-1)

    kv = jnp.concatenate([keys, values], axis=0)
    kv_from = [passed_along(kv, "ctx", 2**m) for m in levels]
    q_from = [passed_along(queries, "ctx", -(2**m)) for m in levels]

    grad_att = lax.dot_general(
        lax.all_gather(d_out, "head", axis=1, tiled=True),
        out_weight,
        (((1,), (1,)), ((), ())),
        preferred_element_type=jnp.float32,
    )
    g = grad_att.astype(jnp.bfloat16)
    g_from = [passed_along(g, "ctx", -(2**m)) for m in levels]
    weight_cols = lax.all_to_all(out_weight, "head", 1, 0, tiled=True)
    kv_from, q_from, g_from, valid_q, valid_k, weight_cols = lax.optimization_barrier(
        (kv_from, q_from, g_from, valid_q, valid_k, weight_cols)
    )

    attended, query_grad, stats = query_call(
        valid_q, queries, g, keys, values, kv_from, heads_local, n_levels
    )
    output = jnp.dot(
        lax.all_gather(attended, "head", axis=1, tiled=True),
        weight_cols,
        preferred_element_type=jnp.float32,
    ).astype(jnp.bfloat16)

    every = lax.all_to_all(
        jnp.broadcast_to(stats[None], (ctx_count,) + stats.shape), "ctx", 0, 0, tiled=False
    )
    st_from = [
        lax.dynamic_index_in_dim(every, jnp.minimum(ctx_index + 2**m, ctx_count - 1), 0, False)
        for m in levels
    ]
    key_grad, value_grad = key_call(
        valid_k, keys, values, queries, g, stats, q_from, g_from, st_from, heads_local, n_levels
    )
    return output, query_grad, key_grad, value_grad


def solution(mesh):
    return jax.shard_map(
        local,
        mesh=mesh,
        in_specs=(
            P("ctx", "head"),
            P("ctx", "head"),
            P("ctx", "head"),
            P("head", None),
            P("ctx", "head"),
            P(),
            P(),
        ),
        out_specs=(P("ctx", "head"), P("ctx", "head"), P("ctx", "head"), P("ctx", "head")),
        check_vma=False,
    )
```

```python
import functools

import jax
import jax.numpy as jnp
from jax import lax
from jax.experimental import pallas as pl
from jax.experimental.pallas import tpu as pltpu
from jax.sharding import PartitionSpec as P

HD = 128
BLK = 128
WIN_MAX = 3
LEVELS = 5
NB = 4


neg_large = -1e30


def passed_along(block, axis, distance):
    devices = range(lax.axis_size(axis))
    route = [(i - distance, i) for i in devices if i - distance in devices]
    return lax.ppermute(block, axis, route)


def dot_nt(a, b):
    return lax.dot_general(a, b, (((1,), (1,)), ((), ())), preferred_element_type=jnp.float32)


def dot_nn(a, b):
    return jnp.dot(a, b, preferred_element_type=jnp.float32)


def col_to_row(col):
    eye = lax.broadcasted_iota(jnp.int32, (BLK, BLK), 0) == lax.broadcasted_iota(
        jnp.int32, (BLK, BLK), 1
    )
    return jnp.sum(jnp.where(eye, col, 0.0), axis=0, keepdims=True)


def candidate_mask(valid_ref, base, n_cand, diag):
    width = n_cand * BLK
    col = lax.broadcasted_iota(jnp.int32, (BLK, width), 1)
    allowed = (col < BLK) & diag
    for ci in range(1, n_cand):
        inside = (col >= ci * BLK) & (col < (ci + 1) * BLK)
        allowed = allowed | (inside & (valid_ref[base + ci] != 0))
    return allowed


def row_to_col(row):
    eye = lax.broadcasted_iota(jnp.int32, (BLK, BLK), 0) == lax.broadcasted_iota(
        jnp.int32, (BLK, BLK), 1
    )
    return jnp.sum(jnp.where(eye, row, 0.0), axis=1, keepdims=True)


def query_blocks(n_levels, valid_ref, q_ref, k_ref, v_ref, kv_refs):
    kf = kv_refs[0::2]
    vf = kv_refs[1::2]
    n_cand = 1 + WIN_MAX + n_levels
    scale = HD ** (-0.5)
    col = lax.broadcasted_iota(jnp.int32, (BLK, n_cand * BLK), 1)
    row = lax.broadcasted_iota(jnp.int32, (BLK, n_cand * BLK), 0)
    diag = col <= row
    for n in range(NB):
        rows = pl.ds(n * BLK, BLK)
        qn = q_ref[rows, :]
        cands = [(k_ref, v_ref, n)]
        for o in range(1, WIN_MAX + 1):
            j = n - o
            cands.append((k_ref, v_ref, j) if j >= 0 else (kf[0], vf[0], NB + j))
        for mi in range(n_levels):
            cands.append((kf[mi], vf[mi], n))
        kcat = jnp.concatenate([kr[pl.ds(j * BLK, BLK), :] for kr, _, j in cands], axis=0)
        vcat = jnp.concatenate([vr[pl.ds(j * BLK, BLK), :] for _, vr, j in cands], axis=0)
        allowed = candidate_mask(valid_ref, n * n_cand, n_cand, diag)
        scores = jnp.where(allowed, dot_nt(qn, kcat) * scale, neg_large)
        yield n, rows, kcat, vcat, scores


def query_fwd_kernel(n_levels, valid_ref, q_ref, g_ref, k_ref, v_ref, *rest):
    att_ref, st_ref = rest[2 * n_levels :]
    blocks = query_blocks(n_levels, valid_ref, q_ref, k_ref, v_ref, rest[: 2 * n_levels])
    for n, rows, kcat, vcat, scores in blocks:
        row_max = scores.max(axis=1, keepdims=True)
        row_total = jnp.sum(jnp.exp(scores - row_max), axis=1, keepdims=True)
        log_total = row_max + jnp.log(row_total)
        probs = jnp.exp(scores - log_total)
        att_b = dot_nn(probs.astype(jnp.bfloat16), vcat).astype(jnp.bfloat16)
        att_ref[rows, :] = att_b
        gn = g_ref[rows, :]
        delta = jnp.sum(gn.astype(jnp.float32) * att_b.astype(jnp.float32), axis=1, keepdims=True)
        st_ref[0, 0, pl.ds(n, 1), :] = col_to_row(log_total)
        st_ref[1, 0, pl.ds(n, 1), :] = col_to_row(delta)


def query_bwd_kernel(n_levels, valid_ref, q_ref, g_ref, k_ref, v_ref, st_ref, *rest):
    dq_ref = rest[2 * n_levels]
    scale = HD ** (-0.5)
    blocks = query_blocks(n_levels, valid_ref, q_ref, k_ref, v_ref, rest[: 2 * n_levels])
    for n, rows, kcat, vcat, scores in blocks:
        log_total = row_to_col(st_ref[0, 0, pl.ds(n, 1), :])
        delta = row_to_col(st_ref[1, 0, pl.ds(n, 1), :])
        probs = jnp.exp(scores - log_total)
        d_prob = dot_nt(g_ref[rows, :], vcat)
        d_score = (probs * (d_prob - delta) * scale).astype(jnp.bfloat16)
        dq_ref[rows, :] = dot_nn(d_score, kcat).astype(jnp.bfloat16)


def key_kernel(n_levels, valid_ref, k_ref, v_ref, q_ref, g_ref, st_ref, *rest):
    qf = rest[0 : 3 * n_levels : 3]
    gf = rest[1 : 3 * n_levels : 3]
    sf = rest[2 : 3 * n_levels : 3]
    dk_ref, dv_ref = rest[3 * n_levels :]
    n_cand = 1 + WIN_MAX + n_levels
    width = n_cand * BLK
    scale = HD ** (-0.5)
    col = lax.broadcasted_iota(jnp.int32, (BLK, width), 1)
    row = lax.broadcasted_iota(jnp.int32, (BLK, width), 0)
    diag = row <= col
    for j in range(NB):
        rows = pl.ds(j * BLK, BLK)
        kj = k_ref[rows, :]
        vj = v_ref[rows, :]
        cands = [(q_ref, g_ref, st_ref, j)]
        for o in range(1, WIN_MAX + 1):
            i = j + o
            cands.append((q_ref, g_ref, st_ref, i) if i < NB else (qf[0], gf[0], sf[0], i - NB))
        for mi in range(n_levels):
            cands.append((qf[mi], gf[mi], sf[mi], j))
        qcat = jnp.concatenate([qr[pl.ds(i * BLK, BLK), :] for qr, _, _, i in cands], axis=0)
        gcat = jnp.concatenate([gr[pl.ds(i * BLK, BLK), :] for _, gr, _, i in cands], axis=0)
        lse = jnp.concatenate([sr[0, 0, pl.ds(i, 1), :] for _, _, sr, i in cands], axis=1)
        delta = jnp.concatenate([sr[1, 0, pl.ds(i, 1), :] for _, _, sr, i in cands], axis=1)
        allowed = candidate_mask(valid_ref, j * n_cand, n_cand, diag)
        scores = jnp.where(allowed, dot_nt(kj, qcat) * scale, neg_large)
        probs = jnp.exp(scores - lse)
        dv_ref[rows, :] = dot_nn(probs.astype(jnp.bfloat16), gcat).astype(jnp.bfloat16)
        d_prob = dot_nt(vj, gcat)
        d_score = (probs * (d_prob - delta) * scale).astype(jnp.bfloat16)
        dk_ref[rows, :] = dot_nn(d_score, qcat).astype(jnp.bfloat16)


def head_block(part):
    return pl.BlockSpec((NB * BLK, HD), lambda h, valid: (part, h))


def stats_block(heads):
    return pl.BlockSpec((2, 1, NB, BLK), lambda h, valid: (0, h, 0, 0))


def query_call(kernel, valid, q, g, k, v, kv_from, extra, heads, n_levels, out_specs, out_shape, name):
    in_specs = [head_block(0)] * 4 + [stats_block(heads)] * len(extra)
    args = [q, g, k, v] + list(extra)
    for kv in kv_from:
        in_specs += [head_block(0), head_block(1)]
        args += [kv, kv]
    grid_spec = pltpu.PrefetchScalarGridSpec(
        num_scalar_prefetch=1,
        grid=(heads,),
        in_specs=in_specs,
        out_specs=out_specs,
    )
    return pl.pallas_call(
        functools.partial(kernel, n_levels),
        grid_spec=grid_spec,
        out_shape=out_shape,
        name=name,
    )(valid, *args)


def key_call(valid, k, v, q, g, stats, q_from, g_from, st_from, heads, n_levels):
    tokens, features = q.shape
    in_specs = [head_block(0)] * 4 + [stats_block(heads)]
    args = [k, v, q, g, stats]
    for qa, ga, st in zip(q_from, g_from, st_from):
        in_specs += [head_block(0), head_block(0), stats_block(heads)]
        args += [qa, ga, st]
    grid_spec = pltpu.PrefetchScalarGridSpec(
        num_scalar_prefetch=1,
        grid=(heads,),
        in_specs=in_specs,
        out_specs=[head_block(0), head_block(0)],
    )
    return pl.pallas_call(
        functools.partial(key_kernel, n_levels),
        grid_spec=grid_spec,
        out_shape=[
            jax.ShapeDtypeStruct((tokens, features), jnp.bfloat16),
            jax.ShapeDtypeStruct((tokens, features), jnp.bfloat16),
        ],
        name="key_side",
    )(valid, *args)


def local(queries, keys, values, out_weight, d_out, window, far_select):
    tokens_local = queries.shape[0]
    heads_local = queries.shape[1] // HD
    assert tokens_local == NB * BLK
    ctx_count = lax.axis_size("ctx")
    ctx_index = lax.axis_index("ctx")
    nblocks = ctx_count * NB
    last = nblocks - 1
    levels = [m for m in range(LEVELS) if 2**m < ctx_count]
    n_levels = len(levels)
    block_ids = ctx_index * NB + jnp.arange(NB, dtype=jnp.int32)

    own_window = lax.dynamic_slice_in_dim(window, ctx_index * NB, NB, 0)
    own_select = lax.dynamic_slice_in_dim(far_select, ctx_index * NB, NB, 0)
    valid_cols = [block_ids >= 0]
    for offset in range(1, WIN_MAX + 1):
        valid_cols.append((offset <= own_window) & (block_ids - offset >= 0))
    for m in levels:
        valid_cols.append((own_select[:, m] == 1) & (block_ids - NB * 2**m >= 0))
    valid_q = jnp.stack(valid_cols, axis=1).astype(jnp.int32).reshape(-1)

    key_cols = [block_ids >= 0]
    for offset in range(1, WIN_MAX + 1):
        qb = block_ids + offset
        key_cols.append((qb <= last) & (offset <= jnp.take(window, jnp.minimum(qb, last))))
    for m in levels:
        qb = block_ids + NB * 2**m
        key_cols.append((qb <= last) & (jnp.take(far_select[:, m], jnp.minimum(qb, last)) == 1))
    valid_k = jnp.stack(key_cols, axis=1).astype(jnp.int32).reshape(-1)

    kv = jnp.concatenate([keys, values], axis=0)
    kv_from = [passed_along(kv, "ctx", 2**m) for m in levels]
    q_from = [passed_along(queries, "ctx", -(2**m)) for m in levels]

    grad_att = lax.dot_general(
        lax.all_gather(d_out, "head", axis=1, tiled=True),
        out_weight,
        (((1,), (1,)), ((), ())),
        preferred_element_type=jnp.float32,
    )
    g = grad_att.astype(jnp.bfloat16)
    g_from = [passed_along(g, "ctx", -(2**m)) for m in levels]
    weight_cols = lax.all_to_all(out_weight, "head", 1, 0, tiled=True)
    kv_from, q_from, g_from, valid_q, valid_k, weight_cols = lax.optimization_barrier(
        (kv_from, q_from, g_from, valid_q, valid_k, weight_cols)
    )

    flat = jax.ShapeDtypeStruct(queries.shape, jnp.bfloat16)
    stats_shape = jax.ShapeDtypeStruct((2, heads_local, NB, BLK), jnp.float32)
    attended, stats = query_call(
        query_fwd_kernel, valid_q, queries, g, keys, values, kv_from, [], heads_local, n_levels,
        [head_block(0), stats_block(heads_local)], [flat, stats_shape], "query_forward",
    )
    (query_grad,) = query_call(
        query_bwd_kernel, valid_q, queries, g, keys, values, kv_from, [stats], heads_local,
        n_levels, [head_block(0)], [flat], "query_backward",
    )
    output = jnp.dot(
        lax.all_gather(attended, "head", axis=1, tiled=True),
        weight_cols,
        preferred_element_type=jnp.float32,
    ).astype(jnp.bfloat16)

    every = lax.all_to_all(
        jnp.broadcast_to(stats[None], (ctx_count,) + stats.shape), "ctx", 0, 0, tiled=False
    )
    st_from = [
        lax.dynamic_index_in_dim(every, jnp.minimum(ctx_index + 2**m, ctx_count - 1), 0, False)
        for m in levels
    ]
    key_grad, value_grad = key_call(
        valid_k, keys, values, queries, g, stats, q_from, g_from, st_from, heads_local, n_levels
    )
    return output, query_grad, key_grad, value_grad


def solution(mesh):
    return jax.shard_map(
        local,
        mesh=mesh,
        in_specs=(
            P("ctx", "head"),
            P("ctx", "head"),
            P("ctx", "head"),
            P("head", None),
            P("ctx", "head"),
            P(),
            P(),
        ),
        out_specs=(P("ctx", "head"), P("ctx", "head"), P("ctx", "head"), P("ctx", "head")),
        check_vma=False,
    )
```

```python
import functools

import jax
import jax.numpy as jnp
from jax import lax
from jax.experimental import pallas as pl
from jax.experimental.pallas import tpu as pltpu
from jax.sharding import PartitionSpec as P

HD = 128
BLK = 128
WIN_MAX = 3
LEVELS = 5
NB = 4


neg_large = -1e30


def passed_along(block, axis, distance):
    devices = range(lax.axis_size(axis))
    route = [(i - distance, i) for i in devices if i - distance in devices]
    return lax.ppermute(block, axis, route)


def dot_nt(a, b):
    return lax.dot_general(a, b, (((1,), (1,)), ((), ())), preferred_element_type=jnp.float32)


def dot_nn(a, b):
    return jnp.dot(a, b, preferred_element_type=jnp.float32)


def col_to_row(col):
    eye = lax.broadcasted_iota(jnp.int32, (BLK, BLK), 0) == lax.broadcasted_iota(
        jnp.int32, (BLK, BLK), 1
    )
    return jnp.sum(jnp.where(eye, col, 0.0), axis=0, keepdims=True)


def candidate_mask(valid_ref, base, n_cand, diag):
    width = n_cand * BLK
    col = lax.broadcasted_iota(jnp.int32, (BLK, width), 1)
    allowed = (col < BLK) & diag
    for ci in range(1, n_cand):
        inside = (col >= ci * BLK) & (col < (ci + 1) * BLK)
        allowed = allowed | (inside & (valid_ref[base + ci] != 0))
    return allowed


def query_kernel(n_levels, valid_ref, q_ref, g_ref, k_ref, v_ref, *rest):
    kf = rest[0 : 2 * n_levels : 2]
    vf = rest[1 : 2 * n_levels : 2]
    att_ref, dq_ref, st_ref = rest[2 * n_levels :]
    n_cand = 1 + WIN_MAX + n_levels
    width = n_cand * BLK
    scale = HD ** (-0.5)
    col = lax.broadcasted_iota(jnp.int32, (BLK, width), 1)
    row = lax.broadcasted_iota(jnp.int32, (BLK, width), 0)
    diag = col <= row
    for n in range(NB):
        rows = pl.ds(n * BLK, BLK)
        qn = q_ref[rows, :]
        gn = g_ref[rows, :]
        cands = [(k_ref, v_ref, n)]
        for o in range(1, WIN_MAX + 1):
            j = n - o
            cands.append((k_ref, v_ref, j) if j >= 0 else (kf[0], vf[0], NB + j))
        for mi in range(n_levels):
            cands.append((kf[mi], vf[mi], n))
        kcat = jnp.concatenate([kr[pl.ds(j * BLK, BLK), :] for kr, _, j in cands], axis=0)
        vcat = jnp.concatenate([vr[pl.ds(j * BLK, BLK), :] for _, vr, j in cands], axis=0)
        allowed = candidate_mask(valid_ref, n * n_cand, n_cand, diag)
        scores = jnp.where(allowed, dot_nt(qn, kcat) * scale, neg_large)
        row_max = scores.max(axis=1, keepdims=True)
        shifted = jnp.exp(scores - row_max)
        row_total = jnp.sum(shifted, axis=1, keepdims=True)
        log_total = row_max + jnp.log(row_total)
        probs = shifted * (1.0 / row_total)
        att_b = dot_nn(probs.astype(jnp.bfloat16), vcat).astype(jnp.bfloat16)
        att_ref[rows, :] = att_b
        delta = jnp.sum(gn.astype(jnp.float32) * att_b.astype(jnp.float32), axis=1, keepdims=True)
        d_prob = dot_nt(gn, vcat)
        d_score = (probs * (d_prob - delta) * scale).astype(jnp.bfloat16)
        dq_ref[rows, :] = dot_nn(d_score, kcat).astype(jnp.bfloat16)
        st_ref[0, 0, pl.ds(n, 1), :] = col_to_row(log_total)
        st_ref[1, 0, pl.ds(n, 1), :] = col_to_row(delta)


def key_kernel(n_levels, valid_ref, k_ref, v_ref, q_ref, g_ref, st_ref, *rest):
    qf = rest[0 : 3 * n_levels : 3]
    gf = rest[1 : 3 * n_levels : 3]
    sf = rest[2 : 3 * n_levels : 3]
    dk_ref, dv_ref = rest[3 * n_levels :]
    n_cand = 1 + WIN_MAX + n_levels
    width = n_cand * BLK
    scale = HD ** (-0.5)
    col = lax.broadcasted_iota(jnp.int32, (BLK, width), 1)
    row = lax.broadcasted_iota(jnp.int32, (BLK, width), 0)
    diag = row <= col
    for j in range(NB):
        rows = pl.ds(j * BLK, BLK)
        kj = k_ref[rows, :]
        vj = v_ref[rows, :]
        cands = [(q_ref, g_ref, st_ref, j)]
        for o in range(1, WIN_MAX + 1):
            i = j + o
            cands.append((q_ref, g_ref, st_ref, i) if i < NB else (qf[0], gf[0], sf[0], i - NB))
        for mi in range(n_levels):
            cands.append((qf[mi], gf[mi], sf[mi], j))
        qcat = jnp.concatenate([qr[pl.ds(i * BLK, BLK), :] for qr, _, _, i in cands], axis=0)
        gcat = jnp.concatenate([gr[pl.ds(i * BLK, BLK), :] for _, gr, _, i in cands], axis=0)
        lse = jnp.concatenate([sr[0, 0, pl.ds(i, 1), :] for _, _, sr, i in cands], axis=1)
        delta = jnp.concatenate([sr[1, 0, pl.ds(i, 1), :] for _, _, sr, i in cands], axis=1)
        allowed = candidate_mask(valid_ref, j * n_cand, n_cand, diag)
        scores = jnp.where(allowed, dot_nt(kj, qcat) * scale, neg_large)
        probs = jnp.exp(scores - lse)
        dv_ref[rows, :] = dot_nn(probs.astype(jnp.bfloat16), gcat).astype(jnp.bfloat16)
        d_prob = dot_nt(vj, gcat)
        d_score = (probs * (d_prob - delta) * scale).astype(jnp.bfloat16)
        dk_ref[rows, :] = dot_nn(d_score, qcat).astype(jnp.bfloat16)


def head_block(part):
    return pl.BlockSpec((NB * BLK, HD), lambda h, valid: (part, h))


def stats_block(heads):
    return pl.BlockSpec((2, 1, NB, BLK), lambda h, valid: (0, h, 0, 0))


def query_call(valid, q, g, k, v, kv_from, heads, n_levels):
    tokens, features = q.shape
    in_specs = [head_block(0)] * 4
    args = [q, g, k, v]
    for kv in kv_from:
        in_specs += [head_block(0), head_block(1)]
        args += [kv, kv]
    grid_spec = pltpu.PrefetchScalarGridSpec(
        num_scalar_prefetch=1,
        grid=(heads,),
        in_specs=in_specs,
        out_specs=[head_block(0), head_block(0), stats_block(heads)],
    )
    return pl.pallas_call(
        functools.partial(query_kernel, n_levels),
        grid_spec=grid_spec,
        out_shape=[
            jax.ShapeDtypeStruct((tokens, features), jnp.bfloat16),
            jax.ShapeDtypeStruct((tokens, features), jnp.bfloat16),
            jax.ShapeDtypeStruct((2, heads, NB, BLK), jnp.float32),
        ],
        name="query_side",
    )(valid, *args)


def key_call(valid, k, v, q, g, stats, q_from, g_from, st_from, heads, n_levels):
    tokens, features = q.shape
    in_specs = [head_block(0)] * 4 + [stats_block(heads)]
    args = [k, v, q, g, stats]
    for qa, ga, st in zip(q_from, g_from, st_from):
        in_specs += [head_block(0), head_block(0), stats_block(heads)]
        args += [qa, ga, st]
    grid_spec = pltpu.PrefetchScalarGridSpec(
        num_scalar_prefetch=1,
        grid=(heads,),
        in_specs=in_specs,
        out_specs=[head_block(0), head_block(0)],
    )
    return pl.pallas_call(
        functools.partial(key_kernel, n_levels),
        grid_spec=grid_spec,
        out_shape=[
            jax.ShapeDtypeStruct((tokens, features), jnp.bfloat16),
            jax.ShapeDtypeStruct((tokens, features), jnp.bfloat16),
        ],
        name="key_side",
    )(valid, *args)


def local(queries, keys, values, out_weight, d_out, window, far_select):
    tokens_local = queries.shape[0]
    heads_local = queries.shape[1] // HD
    assert tokens_local == NB * BLK
    ctx_count = lax.axis_size("ctx")
    ctx_index = lax.axis_index("ctx")
    nblocks = ctx_count * NB
    last = nblocks - 1
    levels = [m for m in range(LEVELS) if 2**m < ctx_count]
    n_levels = len(levels)
    block_ids = ctx_index * NB + jnp.arange(NB, dtype=jnp.int32)

    own_window = lax.dynamic_slice_in_dim(window, ctx_index * NB, NB, 0)
    own_select = lax.dynamic_slice_in_dim(far_select, ctx_index * NB, NB, 0)
    valid_cols = [block_ids >= 0]
    for offset in range(1, WIN_MAX + 1):
        valid_cols.append((offset <= own_window) & (block_ids - offset >= 0))
    for m in levels:
        valid_cols.append((own_select[:, m] == 1) & (block_ids - NB * 2**m >= 0))
    valid_q = jnp.stack(valid_cols, axis=1).astype(jnp.int32).reshape(-1)

    key_cols = [block_ids >= 0]
    for offset in range(1, WIN_MAX + 1):
        qb = block_ids + offset
        key_cols.append((qb <= last) & (offset <= jnp.take(window, jnp.minimum(qb, last))))
    for m in levels:
        qb = block_ids + NB * 2**m
        key_cols.append((qb <= last) & (jnp.take(far_select[:, m], jnp.minimum(qb, last)) == 1))
    valid_k = jnp.stack(key_cols, axis=1).astype(jnp.int32).reshape(-1)

    kv = jnp.concatenate([keys, values], axis=0)
    kv_from = [passed_along(kv, "ctx", 2**m) for m in levels]
    q_from = [passed_along(queries, "ctx", -(2**m)) for m in levels]

    grad_att = lax.dot_general(
        lax.all_gather(d_out, "head", axis=1, tiled=True),
        out_weight,
        (((1,), (1,)), ((), ())),
        preferred_element_type=jnp.float32,
    )
    g = grad_att.astype(jnp.bfloat16)
    g_from = [passed_along(g, "ctx", -(2**m)) for m in levels]
    weight_cols = lax.all_to_all(out_weight, "head", 1, 0, tiled=True)
    kv_from, q_from, g_from, valid_q, valid_k, weight_cols = lax.optimization_barrier(
        (kv_from, q_from, g_from, valid_q, valid_k, weight_cols)
    )

    attended, query_grad, stats = query_call(
        valid_q, queries, g, keys, values, kv_from, heads_local, n_levels
    )
    output = jnp.dot(
        lax.all_gather(attended, "head", axis=1, tiled=True),
        weight_cols,
        preferred_element_type=jnp.float32,
    ).astype(jnp.bfloat16)

    st_from = [passed_along(stats, "ctx", -(2**m)) for m in levels]
    key_grad, value_grad = key_call(
        valid_k, keys, values, queries, g, stats, q_from, g_from, st_from, heads_local, n_levels
    )
    return output, query_grad, key_grad, value_grad


def solution(mesh):
    return jax.shard_map(
        local,
        mesh=mesh,
        in_specs=(
            P("ctx", "head"),
            P("ctx", "head"),
            P("ctx", "head"),
            P("head", None),
            P("ctx", "head"),
            P(),
            P(),
        ),
        out_specs=(P("ctx", "head"), P("ctx", "head"), P("ctx", "head"), P("ctx", "head")),
        check_vma=False,
    )
```

```python
import functools

import jax
import jax.numpy as jnp
from jax import lax
from jax.experimental import pallas as pl
from jax.experimental.pallas import tpu as pltpu
from jax.sharding import PartitionSpec as P

HD = 128
BLK = 128
WIN_MAX = 3
LEVELS = 5
NB = 4


neg_large = -1e30


def passed_along(block, axis, distance):
    devices = range(lax.axis_size(axis))
    route = [(i - distance, i) for i in devices if i - distance in devices]
    return lax.ppermute(block, axis, route)


def dot_nt(a, b):
    return lax.dot_general(a, b, (((1,), (1,)), ((), ())), preferred_element_type=jnp.float32)


def dot_nn(a, b):
    return jnp.dot(a, b, preferred_element_type=jnp.float32)


def col_to_row(col):
    eye = lax.broadcasted_iota(jnp.int32, (BLK, BLK), 0) == lax.broadcasted_iota(
        jnp.int32, (BLK, BLK), 1
    )
    return jnp.sum(jnp.where(eye, col, 0.0), axis=0, keepdims=True)


def candidate_mask(valid_ref, base, n_cand, diag):
    width = n_cand * BLK
    col = lax.broadcasted_iota(jnp.int32, (BLK, width), 1)
    allowed = (col < BLK) & diag
    for ci in range(1, n_cand):
        inside = (col >= ci * BLK) & (col < (ci + 1) * BLK)
        allowed = allowed | (inside & (valid_ref[base + ci] != 0))
    return allowed


def query_kernel(n_levels, valid_ref, q_ref, g_ref, k_ref, v_ref, *rest):
    kf = rest[0 : 2 * n_levels : 2]
    vf = rest[1 : 2 * n_levels : 2]
    att_ref, dq_ref, st_ref = rest[2 * n_levels :]
    n_cand = 1 + WIN_MAX + n_levels
    width = n_cand * BLK
    scale = HD ** (-0.5)
    col = lax.broadcasted_iota(jnp.int32, (BLK, width), 1)
    row = lax.broadcasted_iota(jnp.int32, (BLK, width), 0)
    diag = col <= row
    for n in range(NB):
        rows = pl.ds(n * BLK, BLK)
        qn = q_ref[rows, :]
        gn = g_ref[rows, :]
        cands = [(k_ref, v_ref, n)]
        for o in range(1, WIN_MAX + 1):
            j = n - o
            cands.append((k_ref, v_ref, j) if j >= 0 else (kf[0], vf[0], NB + j))
        for mi in range(n_levels):
            cands.append((kf[mi], vf[mi], n))
        kcat = jnp.concatenate([kr[pl.ds(j * BLK, BLK), :] for kr, _, j in cands], axis=0)
        vcat = jnp.concatenate([vr[pl.ds(j * BLK, BLK), :] for _, vr, j in cands], axis=0)
        allowed = candidate_mask(valid_ref, n * n_cand, n_cand, diag)
        scores = jnp.where(allowed, dot_nt(qn, kcat) * scale, neg_large)
        row_max = scores.max(axis=1, keepdims=True)
        shifted = jnp.exp(scores - row_max)
        row_total = jnp.sum(shifted, axis=1, keepdims=True)
        log_total = row_max + jnp.log(row_total)
        probs = shifted * (1.0 / row_total)
        att_b = dot_nn(probs.astype(jnp.bfloat16), vcat).astype(jnp.bfloat16)
        att_ref[rows, :] = att_b
        delta = jnp.sum(gn.astype(jnp.float32) * att_b.astype(jnp.float32), axis=1, keepdims=True)
        d_prob = dot_nt(gn, vcat)
        d_score = (probs * (d_prob - delta) * scale).astype(jnp.bfloat16)
        dq_ref[rows, :] = dot_nn(d_score, kcat).astype(jnp.bfloat16)
        st_ref[0, 0, pl.ds(n, 1), :] = col_to_row(log_total)
        st_ref[1, 0, pl.ds(n, 1), :] = col_to_row(delta)


def key_kernel(n_levels, valid_ref, k_ref, v_ref, q_ref, g_ref, st_ref, *rest):
    qf = rest[0 : 3 * n_levels : 3]
    gf = rest[1 : 3 * n_levels : 3]
    sf = rest[2 : 3 * n_levels : 3]
    dk_ref, dv_ref = rest[3 * n_levels :]
    n_cand = 1 + WIN_MAX + n_levels
    width = n_cand * BLK
    scale = HD ** (-0.5)
    col = lax.broadcasted_iota(jnp.int32, (BLK, width), 1)
    row = lax.broadcasted_iota(jnp.int32, (BLK, width), 0)
    diag = row <= col
    for j in range(NB):
        rows = pl.ds(j * BLK, BLK)
        kj = k_ref[rows, :]
        vj = v_ref[rows, :]
        cands = [(q_ref, g_ref, st_ref, j)]
        for o in range(1, WIN_MAX + 1):
            i = j + o
            cands.append((q_ref, g_ref, st_ref, i) if i < NB else (qf[0], gf[0], sf[0], i - NB))
        for mi in range(n_levels):
            cands.append((qf[mi], gf[mi], sf[mi], j))
        qcat = jnp.concatenate([qr[pl.ds(i * BLK, BLK), :] for qr, _, _, i in cands], axis=0)
        gcat = jnp.concatenate([gr[pl.ds(i * BLK, BLK), :] for _, gr, _, i in cands], axis=0)
        lse = jnp.concatenate([sr[0, 0, pl.ds(i, 1), :] for _, _, sr, i in cands], axis=1)
        delta = jnp.concatenate([sr[1, 0, pl.ds(i, 1), :] for _, _, sr, i in cands], axis=1)
        allowed = candidate_mask(valid_ref, j * n_cand, n_cand, diag)
        scores = jnp.where(allowed, dot_nt(kj, qcat) * scale, neg_large)
        probs = jnp.exp(scores - lse)
        dv_ref[rows, :] = dot_nn(probs.astype(jnp.bfloat16), gcat).astype(jnp.bfloat16)
        d_prob = dot_nt(vj, gcat)
        d_score = (probs * (d_prob - delta) * scale).astype(jnp.bfloat16)
        dk_ref[rows, :] = dot_nn(d_score, qcat).astype(jnp.bfloat16)


def stack_kernel(a_ref, b_ref, out_ref, sems):
    rows = a_ref.shape[0]
    first = pltpu.make_async_copy(a_ref, out_ref.at[pl.ds(0, rows)], sems.at[0])
    second = pltpu.make_async_copy(b_ref, out_ref.at[pl.ds(rows, rows)], sems.at[1])
    first.start()
    second.start()
    first.wait()
    second.wait()


def stacked_rows(a, b):
    return pl.pallas_call(
        stack_kernel,
        in_specs=[pl.BlockSpec(memory_space=pl.ANY)] * 2,
        out_specs=pl.BlockSpec(memory_space=pl.ANY),
        out_shape=jax.ShapeDtypeStruct((2 * a.shape[0], a.shape[1]), a.dtype),
        scratch_shapes=[pltpu.SemaphoreType.DMA((2,))],
        name="stack_rows",
    )(a, b)


def head_block(part):
    return pl.BlockSpec((NB * BLK, HD), lambda h, valid: (part, h))


def stats_block(heads):
    return pl.BlockSpec((2, 1, NB, BLK), lambda h, valid: (0, h, 0, 0))


def query_call(valid, q, g, k, v, kv_from, heads, n_levels):
    tokens, features = q.shape
    in_specs = [head_block(0)] * 4
    args = [q, g, k, v]
    for kv in kv_from:
        in_specs += [head_block(0), head_block(1)]
        args += [kv, kv]
    grid_spec = pltpu.PrefetchScalarGridSpec(
        num_scalar_prefetch=1,
        grid=(heads,),
        in_specs=in_specs,
        out_specs=[head_block(0), head_block(0), stats_block(heads)],
    )
    return pl.pallas_call(
        functools.partial(query_kernel, n_levels),
        grid_spec=grid_spec,
        out_shape=[
            jax.ShapeDtypeStruct((tokens, features), jnp.bfloat16),
            jax.ShapeDtypeStruct((tokens, features), jnp.bfloat16),
            jax.ShapeDtypeStruct((2, heads, NB, BLK), jnp.float32),
        ],
        name="query_side",
    )(valid, *args)


def key_call(valid, k, v, q, g, stats, q_from, g_from, st_from, heads, n_levels):
    tokens, features = q.shape
    in_specs = [head_block(0)] * 4 + [stats_block(heads)]
    args = [k, v, q, g, stats]
    for qa, ga, st in zip(q_from, g_from, st_from):
        in_specs += [head_block(0), head_block(0), stats_block(heads)]
        args += [qa, ga, st]
    grid_spec = pltpu.PrefetchScalarGridSpec(
        num_scalar_prefetch=1,
        grid=(heads,),
        in_specs=in_specs,
        out_specs=[head_block(0), head_block(0)],
    )
    return pl.pallas_call(
        functools.partial(key_kernel, n_levels),
        grid_spec=grid_spec,
        out_shape=[
            jax.ShapeDtypeStruct((tokens, features), jnp.bfloat16),
            jax.ShapeDtypeStruct((tokens, features), jnp.bfloat16),
        ],
        name="key_side",
    )(valid, *args)


def local(queries, keys, values, out_weight, d_out, window, far_select):
    tokens_local = queries.shape[0]
    heads_local = queries.shape[1] // HD
    assert tokens_local == NB * BLK
    ctx_count = lax.axis_size("ctx")
    ctx_index = lax.axis_index("ctx")
    nblocks = ctx_count * NB
    last = nblocks - 1
    levels = [m for m in range(LEVELS) if 2**m < ctx_count]
    n_levels = len(levels)
    block_ids = ctx_index * NB + jnp.arange(NB, dtype=jnp.int32)

    own_window = lax.dynamic_slice_in_dim(window, ctx_index * NB, NB, 0)
    own_select = lax.dynamic_slice_in_dim(far_select, ctx_index * NB, NB, 0)
    valid_cols = [block_ids >= 0]
    for offset in range(1, WIN_MAX + 1):
        valid_cols.append((offset <= own_window) & (block_ids - offset >= 0))
    for m in levels:
        valid_cols.append((own_select[:, m] == 1) & (block_ids - NB * 2**m >= 0))
    valid_q = jnp.stack(valid_cols, axis=1).astype(jnp.int32).reshape(-1)

    key_cols = [block_ids >= 0]
    for offset in range(1, WIN_MAX + 1):
        qb = block_ids + offset
        key_cols.append((qb <= last) & (offset <= jnp.take(window, jnp.minimum(qb, last))))
    for m in levels:
        qb = block_ids + NB * 2**m
        key_cols.append((qb <= last) & (jnp.take(far_select[:, m], jnp.minimum(qb, last)) == 1))
    valid_k = jnp.stack(key_cols, axis=1).astype(jnp.int32).reshape(-1)

    kv = stacked_rows(keys, values)
    kv_from = [passed_along(kv, "ctx", 2**m) for m in levels]
    q_from = [passed_along(queries, "ctx", -(2**m)) for m in levels]

    grad_att = lax.dot_general(
        lax.all_gather(d_out, "head", axis=1, tiled=True),
        out_weight,
        (((1,), (1,)), ((), ())),
        preferred_element_type=jnp.float32,
    )
    g = grad_att.astype(jnp.bfloat16)
    g_from = [passed_along(g, "ctx", -(2**m)) for m in levels]
    weight_cols = lax.all_to_all(out_weight, "head", 1, 0, tiled=True)
    kv_from, q_from, g_from, valid_q, valid_k, weight_cols = lax.optimization_barrier(
        (kv_from, q_from, g_from, valid_q, valid_k, weight_cols)
    )

    attended, query_grad, stats = query_call(
        valid_q, queries, g, keys, values, kv_from, heads_local, n_levels
    )
    output = jnp.dot(
        lax.all_gather(attended, "head", axis=1, tiled=True),
        weight_cols,
        preferred_element_type=jnp.float32,
    ).astype(jnp.bfloat16)

    st_from = [passed_along(stats, "ctx", -(2**m)) for m in levels]
    key_grad, value_grad = key_call(
        valid_k, keys, values, queries, g, stats, q_from, g_from, st_from, heads_local, n_levels
    )
    return output, query_grad, key_grad, value_grad


def solution(mesh):
    return jax.shard_map(
        local,
        mesh=mesh,
        in_specs=(
            P("ctx", "head"),
            P("ctx", "head"),
            P("ctx", "head"),
            P("head", None),
            P("ctx", "head"),
            P(),
            P(),
        ),
        out_specs=(P("ctx", "head"), P("ctx", "head"), P("ctx", "head"), P("ctx", "head")),
        check_vma=False,
    )
```

```python
import functools

import jax
import jax.numpy as jnp
from jax import lax
from jax.experimental import pallas as pl
from jax.experimental.pallas import tpu as pltpu
from jax.sharding import PartitionSpec as P

HD = 128
BLK = 128
WIN_MAX = 3
LEVELS = 5
NB = 4


neg_large = -1e30


def passed_along(block, axis, distance):
    devices = range(lax.axis_size(axis))
    route = [(i - distance, i) for i in devices if i - distance in devices]
    return lax.ppermute(block, axis, route)


def dot_nt(a, b):
    return lax.dot_general(a, b, (((1,), (1,)), ((), ())), preferred_element_type=jnp.float32)


def dot_nn(a, b):
    return jnp.dot(a, b, preferred_element_type=jnp.float32)


def col_to_row(col):
    eye = lax.broadcasted_iota(jnp.int32, (BLK, BLK), 0) == lax.broadcasted_iota(
        jnp.int32, (BLK, BLK), 1
    )
    return jnp.sum(jnp.where(eye, col, 0.0), axis=0, keepdims=True)


def candidate_mask(valid_ref, base, n_cand, diag):
    width = n_cand * BLK
    col = lax.broadcasted_iota(jnp.int32, (BLK, width), 1)
    allowed = (col < BLK) & diag
    for ci in range(1, n_cand):
        inside = (col >= ci * BLK) & (col < (ci + 1) * BLK)
        allowed = allowed | (inside & (valid_ref[base + ci] != 0))
    return allowed


def query_kernel(n_levels, valid_ref, q_ref, g_ref, k_ref, v_ref, *rest):
    kf = rest[0 : 2 * n_levels : 2]
    vf = rest[1 : 2 * n_levels : 2]
    att_ref, dq_ref, st_ref = rest[2 * n_levels :]
    n_cand = 1 + WIN_MAX + n_levels
    width = n_cand * BLK
    scale = HD ** (-0.5)
    col = lax.broadcasted_iota(jnp.int32, (BLK, width), 1)
    row = lax.broadcasted_iota(jnp.int32, (BLK, width), 0)
    diag = col <= row
    for n in range(NB):
        rows = pl.ds(n * BLK, BLK)
        qn = q_ref[rows, :]
        gn = g_ref[rows, :]
        cands = [(k_ref, v_ref, n)]
        for o in range(1, WIN_MAX + 1):
            j = n - o
            cands.append((k_ref, v_ref, j) if j >= 0 else (kf[0], vf[0], NB + j))
        for mi in range(n_levels):
            cands.append((kf[mi], vf[mi], n))
        kcat = jnp.concatenate([kr[pl.ds(j * BLK, BLK), :] for kr, _, j in cands], axis=0)
        vcat = jnp.concatenate([vr[pl.ds(j * BLK, BLK), :] for _, vr, j in cands], axis=0)
        allowed = candidate_mask(valid_ref, n * n_cand, n_cand, diag)
        scores = jnp.where(allowed, dot_nt(qn, kcat) * scale, neg_large)
        row_max = scores.max(axis=1, keepdims=True)
        shifted = jnp.exp(scores - row_max)
        row_total = jnp.sum(shifted, axis=1, keepdims=True)
        log_total = row_max + jnp.log(row_total)
        probs = shifted * (1.0 / row_total)
        att_b = dot_nn(probs.astype(jnp.bfloat16), vcat).astype(jnp.bfloat16)
        att_ref[rows, :] = att_b
        delta = jnp.sum(gn.astype(jnp.float32) * att_b.astype(jnp.float32), axis=1, keepdims=True)
        d_prob = dot_nt(gn, vcat)
        d_score = (probs * (d_prob - delta) * scale).astype(jnp.bfloat16)
        dq_ref[rows, :] = dot_nn(d_score, kcat).astype(jnp.bfloat16)
        st_ref[0, 0, pl.ds(n, 1), :] = col_to_row(log_total)
        st_ref[1, 0, pl.ds(n, 1), :] = col_to_row(delta)


def key_kernel(n_levels, valid_ref, k_ref, v_ref, q_ref, g_ref, st_ref, *rest):
    qf = rest[0 : 3 * n_levels : 3]
    gf = rest[1 : 3 * n_levels : 3]
    sf = rest[2 : 3 * n_levels : 3]
    dk_ref, dv_ref = rest[3 * n_levels :]
    n_cand = 1 + WIN_MAX + n_levels
    width = n_cand * BLK
    scale = HD ** (-0.5)
    col = lax.broadcasted_iota(jnp.int32, (BLK, width), 1)
    row = lax.broadcasted_iota(jnp.int32, (BLK, width), 0)
    diag = row <= col
    for j in range(NB):
        rows = pl.ds(j * BLK, BLK)
        kj = k_ref[rows, :]
        vj = v_ref[rows, :]
        cands = [(q_ref, g_ref, st_ref, j)]
        for o in range(1, WIN_MAX + 1):
            i = j + o
            cands.append((q_ref, g_ref, st_ref, i) if i < NB else (qf[0], gf[0], sf[0], i - NB))
        for mi in range(n_levels):
            cands.append((qf[mi], gf[mi], sf[mi], j))
        qcat = jnp.concatenate([qr[pl.ds(i * BLK, BLK), :] for qr, _, _, i in cands], axis=0)
        gcat = jnp.concatenate([gr[pl.ds(i * BLK, BLK), :] for _, gr, _, i in cands], axis=0)
        lse = jnp.concatenate([sr[0, 0, pl.ds(i, 1), :] for _, _, sr, i in cands], axis=1)
        delta = jnp.concatenate([sr[1, 0, pl.ds(i, 1), :] for _, _, sr, i in cands], axis=1)
        allowed = candidate_mask(valid_ref, j * n_cand, n_cand, diag)
        scores = jnp.where(allowed, dot_nt(kj, qcat) * scale, neg_large)
        probs = jnp.exp(scores - lse)
        dv_ref[rows, :] = dot_nn(probs.astype(jnp.bfloat16), gcat).astype(jnp.bfloat16)
        d_prob = dot_nt(vj, gcat)
        d_score = (probs * (d_prob - delta) * scale).astype(jnp.bfloat16)
        dk_ref[rows, :] = dot_nn(d_score, qcat).astype(jnp.bfloat16)


def head_block(part):
    return pl.BlockSpec((NB * BLK, HD), lambda h, valid: (part, h))


def stats_block(heads):
    return pl.BlockSpec((2, 1, NB, BLK), lambda h, valid: (0, h, 0, 0))


def query_call(valid, q, g, k, v, kv_from, heads, n_levels):
    tokens, features = q.shape
    in_specs = [head_block(0)] * 4
    args = [q, g, k, v]
    for kv in kv_from:
        in_specs += [head_block(0), head_block(1)]
        args += [kv, kv]
    grid_spec = pltpu.PrefetchScalarGridSpec(
        num_scalar_prefetch=1,
        grid=(heads,),
        in_specs=in_specs,
        out_specs=[head_block(0), head_block(0), stats_block(heads)],
    )
    return pl.pallas_call(
        functools.partial(query_kernel, n_levels),
        grid_spec=grid_spec,
        out_shape=[
            jax.ShapeDtypeStruct((tokens, features), jnp.bfloat16),
            jax.ShapeDtypeStruct((tokens, features), jnp.bfloat16),
            jax.ShapeDtypeStruct((2, heads, NB, BLK), jnp.float32),
        ],
        name="query_side",
    )(valid, *args)


def key_call(valid, k, v, q, g, stats, q_from, g_from, st_from, heads, n_levels):
    tokens, features = q.shape
    in_specs = [head_block(0)] * 4 + [stats_block(heads)]
    args = [k, v, q, g, stats]
    for qa, ga, st in zip(q_from, g_from, st_from):
        in_specs += [head_block(0), head_block(0), stats_block(heads)]
        args += [qa, ga, st]
    grid_spec = pltpu.PrefetchScalarGridSpec(
        num_scalar_prefetch=1,
        grid=(heads,),
        in_specs=in_specs,
        out_specs=[head_block(0), head_block(0)],
    )
    return pl.pallas_call(
        functools.partial(key_kernel, n_levels),
        grid_spec=grid_spec,
        out_shape=[
            jax.ShapeDtypeStruct((tokens, features), jnp.bfloat16),
            jax.ShapeDtypeStruct((tokens, features), jnp.bfloat16),
        ],
        name="key_side",
    )(valid, *args)


def local(queries, keys, values, out_weight, d_out, window, far_select):
    tokens_local = queries.shape[0]
    heads_local = queries.shape[1] // HD
    assert tokens_local == NB * BLK
    ctx_count = lax.axis_size("ctx")
    ctx_index = lax.axis_index("ctx")
    nblocks = ctx_count * NB
    last = nblocks - 1
    levels = [m for m in range(LEVELS) if 2**m < ctx_count]
    n_levels = len(levels)
    block_ids = ctx_index * NB + jnp.arange(NB, dtype=jnp.int32)

    own_window = lax.dynamic_slice_in_dim(window, ctx_index * NB, NB, 0)
    own_select = lax.dynamic_slice_in_dim(far_select, ctx_index * NB, NB, 0)
    valid_cols = [block_ids >= 0]
    for offset in range(1, WIN_MAX + 1):
        valid_cols.append((offset <= own_window) & (block_ids - offset >= 0))
    for m in levels:
        valid_cols.append((own_select[:, m] == 1) & (block_ids - NB * 2**m >= 0))
    valid_q = jnp.stack(valid_cols, axis=1).astype(jnp.int32).reshape(-1)

    key_cols = [block_ids >= 0]
    for offset in range(1, WIN_MAX + 1):
        qb = block_ids + offset
        key_cols.append((qb <= last) & (offset <= jnp.take(window, jnp.minimum(qb, last))))
    for m in levels:
        qb = block_ids + NB * 2**m
        key_cols.append((qb <= last) & (jnp.take(far_select[:, m], jnp.minimum(qb, last)) == 1))
    valid_k = jnp.stack(key_cols, axis=1).astype(jnp.int32).reshape(-1)

    q_from = [passed_along(queries, "ctx", -(2**m)) for m in levels]
    kv = jnp.concatenate([keys, values], axis=0)
    kv, valid_q, valid_k = lax.optimization_barrier((kv, valid_q, valid_k))
    kv_from = [passed_along(kv, "ctx", 2**m) for m in levels]

    grad_att = lax.dot_general(
        lax.all_gather(d_out, "head", axis=1, tiled=True),
        out_weight,
        (((1,), (1,)), ((), ())),
        preferred_element_type=jnp.float32,
    )
    g = grad_att.astype(jnp.bfloat16)
    g_from = [passed_along(g, "ctx", -(2**m)) for m in levels]
    weight_cols = lax.all_to_all(out_weight, "head", 1, 0, tiled=True)
    kv_from, q_from, g_from, valid_q, valid_k, weight_cols = lax.optimization_barrier(
        (kv_from, q_from, g_from, valid_q, valid_k, weight_cols)
    )

    attended, query_grad, stats = query_call(
        valid_q, queries, g, keys, values, kv_from, heads_local, n_levels
    )
    output = jnp.dot(
        lax.all_gather(attended, "head", axis=1, tiled=True),
        weight_cols,
        preferred_element_type=jnp.float32,
    ).astype(jnp.bfloat16)

    st_from = [passed_along(stats, "ctx", -(2**m)) for m in levels]
    key_grad, value_grad = key_call(
        valid_k, keys, values, queries, g, stats, q_from, g_from, st_from, heads_local, n_levels
    )
    return output, query_grad, key_grad, value_grad


def solution(mesh):
    return jax.shard_map(
        local,
        mesh=mesh,
        in_specs=(
            P("ctx", "head"),
            P("ctx", "head"),
            P("ctx", "head"),
            P("head", None),
            P("ctx", "head"),
            P(),
            P(),
        ),
        out_specs=(P("ctx", "head"), P("ctx", "head"), P("ctx", "head"), P("ctx", "head")),
        check_vma=False,
    )
```

```python
import functools

import jax
import jax.numpy as jnp
from jax import lax
from jax.experimental import pallas as pl
from jax.experimental.pallas import tpu as pltpu
from jax.sharding import PartitionSpec as P

HD = 128
BLK = 128
WIN_MAX = 3
LEVELS = 5
NB = 4


neg_large = -1e30


def passed_along(block, axis, distance):
    devices = range(lax.axis_size(axis))
    route = [(i - distance, i) for i in devices if i - distance in devices]
    return lax.ppermute(block, axis, route)


def dot_nt(a, b):
    return lax.dot_general(a, b, (((1,), (1,)), ((), ())), preferred_element_type=jnp.float32)


def dot_nn(a, b):
    return jnp.dot(a, b, preferred_element_type=jnp.float32)


def col_to_row(col):
    eye = lax.broadcasted_iota(jnp.int32, (BLK, BLK), 0) == lax.broadcasted_iota(
        jnp.int32, (BLK, BLK), 1
    )
    return jnp.sum(jnp.where(eye, col, 0.0), axis=0, keepdims=True)


def candidate_mask(valid_ref, base, n_cand, diag):
    width = n_cand * BLK
    col = lax.broadcasted_iota(jnp.int32, (BLK, width), 1)
    allowed = (col < BLK) & diag
    for ci in range(1, n_cand):
        inside = (col >= ci * BLK) & (col < (ci + 1) * BLK)
        allowed = allowed | (inside & (valid_ref[base + ci] != 0))
    return allowed


def query_kernel(n_levels, valid_ref, q_ref, g_ref, k_ref, v_ref, *rest):
    kf = rest[0 : 2 * n_levels : 2]
    vf = rest[1 : 2 * n_levels : 2]
    att_ref, dq_ref, st_ref = rest[2 * n_levels :]
    n_cand = 1 + WIN_MAX + n_levels
    width = n_cand * BLK
    scale = HD ** (-0.5)
    col = lax.broadcasted_iota(jnp.int32, (BLK, width), 1)
    row = lax.broadcasted_iota(jnp.int32, (BLK, width), 0)
    diag = col <= row
    for n in range(NB):
        rows = pl.ds(n * BLK, BLK)
        qn = q_ref[rows, :]
        gn = g_ref[rows, :]
        cands = [(k_ref, v_ref, n)]
        for o in range(1, WIN_MAX + 1):
            j = n - o
            cands.append((k_ref, v_ref, j) if j >= 0 else (kf[0], vf[0], NB + j))
        for mi in range(n_levels):
            cands.append((kf[mi], vf[mi], n))
        kcat = jnp.concatenate([kr[pl.ds(j * BLK, BLK), :] for kr, _, j in cands], axis=0)
        vcat = jnp.concatenate([vr[pl.ds(j * BLK, BLK), :] for _, vr, j in cands], axis=0)
        allowed = candidate_mask(valid_ref, n * n_cand, n_cand, diag)
        scores = jnp.where(allowed, dot_nt(qn, kcat) * scale, neg_large)
        row_max = scores.max(axis=1, keepdims=True)
        shifted = jnp.exp(scores - row_max)
        row_total = jnp.sum(shifted, axis=1, keepdims=True)
        log_total = row_max + jnp.log(row_total)
        probs = shifted * (1.0 / row_total)
        att_b = dot_nn(probs.astype(jnp.bfloat16), vcat).astype(jnp.bfloat16)
        att_ref[rows, :] = att_b
        delta = jnp.sum(gn.astype(jnp.float32) * att_b.astype(jnp.float32), axis=1, keepdims=True)
        d_prob = dot_nt(gn, vcat)
        d_score = (probs * (d_prob - delta) * scale).astype(jnp.bfloat16)
        dq_ref[rows, :] = dot_nn(d_score, kcat).astype(jnp.bfloat16)
        st_ref[0, 0, pl.ds(n, 1), :] = col_to_row(log_total)
        st_ref[1, 0, pl.ds(n, 1), :] = col_to_row(delta)


def key_part_kernel(n_levels, remote, valid_ref, k_ref, v_ref, q_ref, g_ref, st_ref, *rest):
    n_cand = 1 + WIN_MAX + n_levels
    scale = HD ** (-0.5)
    if remote:
        qf = rest[0 : 3 * n_levels : 3]
        gf = rest[1 : 3 * n_levels : 3]
        sf = rest[2 : 3 * n_levels : 3]
        dk_in, dv_in, dk_ref, dv_ref = rest[3 * n_levels :]
    else:
        dk_ref, dv_ref = rest
    for j in range(NB):
        rows = pl.ds(j * BLK, BLK)
        if remote:
            cands = [(qf[0], gf[0], sf[0], j + o - NB, o) for o in range(1, WIN_MAX + 1) if j + o >= NB]
            cands += [(qf[mi], gf[mi], sf[mi], j, 1 + WIN_MAX + mi) for mi in range(n_levels)]
        else:
            cands = [(q_ref, g_ref, st_ref, j, 0)]
            cands += [(q_ref, g_ref, st_ref, j + o, o) for o in range(1, WIN_MAX + 1) if j + o < NB]
        width = len(cands) * BLK
        col = lax.broadcasted_iota(jnp.int32, (BLK, width), 1)
        row = lax.broadcasted_iota(jnp.int32, (BLK, width), 0)
        allowed = None
        for pos, (_, _, _, _, ci) in enumerate(cands):
            inside = (col >= pos * BLK) & (col < (pos + 1) * BLK)
            ok = (row <= col) if ci == 0 else (valid_ref[j * n_cand + ci] != 0)
            term = inside & ok
            allowed = term if allowed is None else allowed | term
        kj = k_ref[rows, :]
        vj = v_ref[rows, :]
        qcat = jnp.concatenate([qr[pl.ds(i * BLK, BLK), :] for qr, _, _, i, _ in cands], axis=0)
        gcat = jnp.concatenate([gr[pl.ds(i * BLK, BLK), :] for _, gr, _, i, _ in cands], axis=0)
        lse = jnp.concatenate([sr[0, 0, pl.ds(i, 1), :] for _, _, sr, i, _ in cands], axis=1)
        delta = jnp.concatenate([sr[1, 0, pl.ds(i, 1), :] for _, _, sr, i, _ in cands], axis=1)
        scores = jnp.where(allowed, dot_nt(kj, qcat) * scale, neg_large)
        probs = jnp.exp(scores - lse)
        dv = dot_nn(probs.astype(jnp.bfloat16), gcat)
        d_prob = dot_nt(vj, gcat)
        d_score = (probs * (d_prob - delta) * scale).astype(jnp.bfloat16)
        dk = dot_nn(d_score, qcat)
        if remote:
            dv_ref[rows, :] = (dv_in[rows, :] + dv).astype(jnp.bfloat16)
            dk_ref[rows, :] = (dk_in[rows, :] + dk).astype(jnp.bfloat16)
        else:
            dv_ref[rows, :] = dv
            dk_ref[rows, :] = dk


def head_block(part):
    return pl.BlockSpec((NB * BLK, HD), lambda h, valid: (part, h))


def stats_block(heads):
    return pl.BlockSpec((2, 1, NB, BLK), lambda h, valid: (0, h, 0, 0))


def query_call(valid, q, g, k, v, kv_from, heads, n_levels):
    tokens, features = q.shape
    in_specs = [head_block(0)] * 4
    args = [q, g, k, v]
    for kv in kv_from:
        in_specs += [head_block(0), head_block(1)]
        args += [kv, kv]
    grid_spec = pltpu.PrefetchScalarGridSpec(
        num_scalar_prefetch=1,
        grid=(heads,),
        in_specs=in_specs,
        out_specs=[head_block(0), head_block(0), stats_block(heads)],
    )
    return pl.pallas_call(
        functools.partial(query_kernel, n_levels),
        grid_spec=grid_spec,
        out_shape=[
            jax.ShapeDtypeStruct((tokens, features), jnp.bfloat16),
            jax.ShapeDtypeStruct((tokens, features), jnp.bfloat16),
            jax.ShapeDtypeStruct((2, heads, NB, BLK), jnp.float32),
        ],
        name="query_side",
    )(valid, *args)


def key_call(valid, k, v, q, g, stats, q_from, g_from, st_from, heads, n_levels):
    tokens, features = q.shape
    in_specs = [head_block(0)] * 4 + [stats_block(heads)]
    args = [k, v, q, g, stats]
    own = pl.pallas_call(
        functools.partial(key_part_kernel, n_levels, False),
        grid_spec=pltpu.PrefetchScalarGridSpec(
            num_scalar_prefetch=1, grid=(heads,), in_specs=in_specs,
            out_specs=[head_block(0), head_block(0)],
        ),
        out_shape=[jax.ShapeDtypeStruct((tokens, features), jnp.float32)] * 2,
        name="key_side_own",
    )(valid, *args)
    for qa, ga, st in zip(q_from, g_from, st_from):
        in_specs += [head_block(0), head_block(0), stats_block(heads)]
        args += [qa, ga, st]
    in_specs += [head_block(0), head_block(0)]
    args += list(own)
    return pl.pallas_call(
        functools.partial(key_part_kernel, n_levels, True),
        grid_spec=pltpu.PrefetchScalarGridSpec(
            num_scalar_prefetch=1, grid=(heads,), in_specs=in_specs,
            out_specs=[head_block(0), head_block(0)],
        ),
        out_shape=[jax.ShapeDtypeStruct((tokens, features), jnp.bfloat16)] * 2,
        name="key_side_remote",
    )(valid, *args)


def local(queries, keys, values, out_weight, d_out, window, far_select):
    tokens_local = queries.shape[0]
    heads_local = queries.shape[1] // HD
    assert tokens_local == NB * BLK
    ctx_count = lax.axis_size("ctx")
    ctx_index = lax.axis_index("ctx")
    nblocks = ctx_count * NB
    last = nblocks - 1
    levels = [m for m in range(LEVELS) if 2**m < ctx_count]
    n_levels = len(levels)
    block_ids = ctx_index * NB + jnp.arange(NB, dtype=jnp.int32)

    own_window = lax.dynamic_slice_in_dim(window, ctx_index * NB, NB, 0)
    own_select = lax.dynamic_slice_in_dim(far_select, ctx_index * NB, NB, 0)
    valid_cols = [block_ids >= 0]
    for offset in range(1, WIN_MAX + 1):
        valid_cols.append((offset <= own_window) & (block_ids - offset >= 0))
    for m in levels:
        valid_cols.append((own_select[:, m] == 1) & (block_ids - NB * 2**m >= 0))
    valid_q = jnp.stack(valid_cols, axis=1).astype(jnp.int32).reshape(-1)

    key_cols = [block_ids >= 0]
    for offset in range(1, WIN_MAX + 1):
        qb = block_ids + offset
        key_cols.append((qb <= last) & (offset <= jnp.take(window, jnp.minimum(qb, last))))
    for m in levels:
        qb = block_ids + NB * 2**m
        key_cols.append((qb <= last) & (jnp.take(far_select[:, m], jnp.minimum(qb, last)) == 1))
    valid_k = jnp.stack(key_cols, axis=1).astype(jnp.int32).reshape(-1)

    kv = jnp.concatenate([keys, values], axis=0)
    kv_from = [passed_along(kv, "ctx", 2**m) for m in levels]
    q_from = [passed_along(queries, "ctx", -(2**m)) for m in levels]

    grad_att = lax.dot_general(
        lax.all_gather(d_out, "head", axis=1, tiled=True),
        out_weight,
        (((1,), (1,)), ((), ())),
        preferred_element_type=jnp.float32,
    )
    g = grad_att.astype(jnp.bfloat16)
    g_from = [passed_along(g, "ctx", -(2**m)) for m in levels]
    weight_cols = lax.all_to_all(out_weight, "head", 1, 0, tiled=True)
    kv_from, q_from, g_from, valid_q, valid_k, weight_cols = lax.optimization_barrier(
        (kv_from, q_from, g_from, valid_q, valid_k, weight_cols)
    )

    attended, query_grad, stats = query_call(
        valid_q, queries, g, keys, values, kv_from, heads_local, n_levels
    )
    output = jnp.dot(
        lax.all_gather(attended, "head", axis=1, tiled=True),
        weight_cols,
        preferred_element_type=jnp.float32,
    ).astype(jnp.bfloat16)

    st_from = [passed_along(stats, "ctx", -(2**m)) for m in levels]
    key_grad, value_grad = key_call(
        valid_k, keys, values, queries, g, stats, q_from, g_from, st_from, heads_local, n_levels
    )
    return output, query_grad, key_grad, value_grad


def solution(mesh):
    return jax.shard_map(
        local,
        mesh=mesh,
        in_specs=(
            P("ctx", "head"),
            P("ctx", "head"),
            P("ctx", "head"),
            P("head", None),
            P("ctx", "head"),
            P(),
            P(),
        ),
        out_specs=(P("ctx", "head"), P("ctx", "head"), P("ctx", "head"), P("ctx", "head")),
        check_vma=False,
    )
```

```python
import functools

import jax
import jax.numpy as jnp
from jax import lax
from jax.experimental import pallas as pl
from jax.experimental.pallas import tpu as pltpu
from jax.sharding import PartitionSpec as P

HD = 128
BLK = 128
WIN_MAX = 3
LEVELS = 5
NB = 4


neg_large = -1e30


def passed_along(block, axis, distance):
    devices = range(lax.axis_size(axis))
    route = [(i - distance, i) for i in devices if i - distance in devices]
    return lax.ppermute(block, axis, route)


def dot_nt(a, b):
    return lax.dot_general(a, b, (((1,), (1,)), ((), ())), preferred_element_type=jnp.float32)


def dot_nn(a, b):
    return jnp.dot(a, b, preferred_element_type=jnp.float32)


def col_to_row(col):
    eye = lax.broadcasted_iota(jnp.int32, (BLK, BLK), 0) == lax.broadcasted_iota(
        jnp.int32, (BLK, BLK), 1
    )
    return jnp.sum(jnp.where(eye, col, 0.0), axis=0, keepdims=True)


def candidate_mask(valid_ref, base, n_cand, diag):
    width = n_cand * BLK
    col = lax.broadcasted_iota(jnp.int32, (BLK, width), 1)
    allowed = (col < BLK) & diag
    for ci in range(1, n_cand):
        inside = (col >= ci * BLK) & (col < (ci + 1) * BLK)
        allowed = allowed | (inside & (valid_ref[base + ci] != 0))
    return allowed


def query_kernel(n_levels, valid_ref, q_ref, g_ref, k_ref, v_ref, *rest):
    kf = rest[0 : 2 * n_levels : 2]
    vf = rest[1 : 2 * n_levels : 2]
    att_ref, dq_ref, st_ref = rest[2 * n_levels :]
    n_cand = 1 + WIN_MAX + n_levels
    width = n_cand * BLK
    scale = HD ** (-0.5)
    col = lax.broadcasted_iota(jnp.int32, (BLK, width), 1)
    row = lax.broadcasted_iota(jnp.int32, (BLK, width), 0)
    diag = col <= row
    for n in range(NB):
        rows = pl.ds(n * BLK, BLK)
        qn = q_ref[rows, :]
        gn = g_ref[rows, :]
        cands = [(k_ref, v_ref, n)]
        for o in range(1, WIN_MAX + 1):
            j = n - o
            cands.append((k_ref, v_ref, j) if j >= 0 else (kf[0], vf[0], NB + j))
        for mi in range(n_levels):
            cands.append((kf[mi], vf[mi], n))
        kcat = jnp.concatenate([kr[pl.ds(j * BLK, BLK), :] for kr, _, j in cands], axis=0)
        vcat = jnp.concatenate([vr[pl.ds(j * BLK, BLK), :] for _, vr, j in cands], axis=0)
        allowed = candidate_mask(valid_ref, n * n_cand, n_cand, diag)
        scores = jnp.where(allowed, dot_nt(qn, kcat) * scale, neg_large)
        row_max = scores.max(axis=1, keepdims=True)
        shifted = jnp.exp(scores - row_max)
        row_total = jnp.sum(shifted, axis=1, keepdims=True)
        log_total = row_max + jnp.log(row_total)
        probs = shifted * (1.0 / row_total)
        att_b = dot_nn(probs.astype(jnp.bfloat16), vcat).astype(jnp.bfloat16)
        att_ref[rows, :] = att_b
        delta = jnp.sum(gn.astype(jnp.float32) * att_b.astype(jnp.float32), axis=1, keepdims=True)
        d_prob = dot_nt(gn, vcat)
        d_score = (probs * (d_prob - delta) * scale).astype(jnp.bfloat16)
        dq_ref[rows, :] = dot_nn(d_score, kcat).astype(jnp.bfloat16)
        st_ref[0, 0, pl.ds(n, 1), :] = col_to_row(log_total)
        st_ref[1, 0, pl.ds(n, 1), :] = col_to_row(delta)


def key_kernel(n_levels, valid_ref, k_ref, v_ref, q_ref, g_ref, st_ref, *rest):
    qf = rest[0 : 3 * n_levels : 3]
    gf = rest[1 : 3 * n_levels : 3]
    sf = rest[2 : 3 * n_levels : 3]
    dk_ref, dv_ref = rest[3 * n_levels :]
    n_cand = 1 + WIN_MAX + n_levels
    width = n_cand * BLK
    scale = HD ** (-0.5)
    col = lax.broadcasted_iota(jnp.int32, (BLK, width), 1)
    row = lax.broadcasted_iota(jnp.int32, (BLK, width), 0)
    diag = row <= col
    for j in range(NB):
        rows = pl.ds(j * BLK, BLK)
        kj = k_ref[rows, :]
        vj = v_ref[rows, :]
        cands = [(q_ref, g_ref, st_ref, j)]
        for o in range(1, WIN_MAX + 1):
            i = j + o
            cands.append((q_ref, g_ref, st_ref, i) if i < NB else (qf[0], gf[0], sf[0], i - NB))
        for mi in range(n_levels):
            cands.append((qf[mi], gf[mi], sf[mi], j))
        qcat = jnp.concatenate([qr[pl.ds(i * BLK, BLK), :] for qr, _, _, i in cands], axis=0)
        gcat = jnp.concatenate([gr[pl.ds(i * BLK, BLK), :] for _, gr, _, i in cands], axis=0)
        lse = jnp.concatenate([sr[0, 0, pl.ds(i, 1), :] for _, _, sr, i in cands], axis=1)
        delta = jnp.concatenate([sr[1, 0, pl.ds(i, 1), :] for _, _, sr, i in cands], axis=1)
        allowed = candidate_mask(valid_ref, j * n_cand, n_cand, diag)
        scores = jnp.where(allowed, dot_nt(kj, qcat) * scale, neg_large)
        probs = jnp.exp(scores - lse)
        dv_ref[rows, :] = dot_nn(probs.astype(jnp.bfloat16), gcat).astype(jnp.bfloat16)
        d_prob = dot_nt(vj, gcat)
        d_score = (probs * (d_prob - delta) * scale).astype(jnp.bfloat16)
        dk_ref[rows, :] = dot_nn(d_score, qcat).astype(jnp.bfloat16)


def project_kernel(a_ref, w_ref, o_ref):
    o_ref[...] = dot_nn(a_ref[...], w_ref[...]).astype(o_ref.dtype)


def projected(a, w):
    rows = a.shape[0]
    tile = BLK if rows % BLK == 0 else rows
    return pl.pallas_call(
        project_kernel,
        grid=(rows // tile,),
        in_specs=[
            pl.BlockSpec((tile, a.shape[1]), lambda i: (i, 0)),
            pl.BlockSpec(w.shape, lambda i: (0, 0)),
        ],
        out_specs=pl.BlockSpec((tile, w.shape[1]), lambda i: (i, 0)),
        out_shape=jax.ShapeDtypeStruct((rows, w.shape[1]), jnp.bfloat16),
        name="output_projection",
    )(a, w)


def head_block(part):
    return pl.BlockSpec((NB * BLK, HD), lambda h, valid: (part, h))


def stats_block(heads):
    return pl.BlockSpec((2, 1, NB, BLK), lambda h, valid: (0, h, 0, 0))


def query_call(valid, q, g, k, v, kv_from, heads, n_levels):
    tokens, features = q.shape
    in_specs = [head_block(0)] * 4
    args = [q, g, k, v]
    for kv in kv_from:
        in_specs += [head_block(0), head_block(1)]
        args += [kv, kv]
    grid_spec = pltpu.PrefetchScalarGridSpec(
        num_scalar_prefetch=1,
        grid=(heads,),
        in_specs=in_specs,
        out_specs=[head_block(0), head_block(0), stats_block(heads)],
    )
    return pl.pallas_call(
        functools.partial(query_kernel, n_levels),
        grid_spec=grid_spec,
        out_shape=[
            jax.ShapeDtypeStruct((tokens, features), jnp.bfloat16),
            jax.ShapeDtypeStruct((tokens, features), jnp.bfloat16),
            jax.ShapeDtypeStruct((2, heads, NB, BLK), jnp.float32),
        ],
        name="query_side",
    )(valid, *args)


def key_call(valid, k, v, q, g, stats, q_from, g_from, st_from, heads, n_levels):
    tokens, features = q.shape
    in_specs = [head_block(0)] * 4 + [stats_block(heads)]
    args = [k, v, q, g, stats]
    for qa, ga, st in zip(q_from, g_from, st_from):
        in_specs += [head_block(0), head_block(0), stats_block(heads)]
        args += [qa, ga, st]
    grid_spec = pltpu.PrefetchScalarGridSpec(
        num_scalar_prefetch=1,
        grid=(heads,),
        in_specs=in_specs,
        out_specs=[head_block(0), head_block(0)],
    )
    return pl.pallas_call(
        functools.partial(key_kernel, n_levels),
        grid_spec=grid_spec,
        out_shape=[
            jax.ShapeDtypeStruct((tokens, features), jnp.bfloat16),
            jax.ShapeDtypeStruct((tokens, features), jnp.bfloat16),
        ],
        name="key_side",
    )(valid, *args)


def local(queries, keys, values, out_weight, d_out, window, far_select):
    tokens_local = queries.shape[0]
    heads_local = queries.shape[1] // HD
    assert tokens_local == NB * BLK
    ctx_count = lax.axis_size("ctx")
    ctx_index = lax.axis_index("ctx")
    nblocks = ctx_count * NB
    last = nblocks - 1
    levels = [m for m in range(LEVELS) if 2**m < ctx_count]
    n_levels = len(levels)
    block_ids = ctx_index * NB + jnp.arange(NB, dtype=jnp.int32)

    own_window = lax.dynamic_slice_in_dim(window, ctx_index * NB, NB, 0)
    own_select = lax.dynamic_slice_in_dim(far_select, ctx_index * NB, NB, 0)
    valid_cols = [block_ids >= 0]
    for offset in range(1, WIN_MAX + 1):
        valid_cols.append((offset <= own_window) & (block_ids - offset >= 0))
    for m in levels:
        valid_cols.append((own_select[:, m] == 1) & (block_ids - NB * 2**m >= 0))
    valid_q = jnp.stack(valid_cols, axis=1).astype(jnp.int32).reshape(-1)

    key_cols = [block_ids >= 0]
    for offset in range(1, WIN_MAX + 1):
        qb = block_ids + offset
        key_cols.append((qb <= last) & (offset <= jnp.take(window, jnp.minimum(qb, last))))
    for m in levels:
        qb = block_ids + NB * 2**m
        key_cols.append((qb <= last) & (jnp.take(far_select[:, m], jnp.minimum(qb, last)) == 1))
    valid_k = jnp.stack(key_cols, axis=1).astype(jnp.int32).reshape(-1)

    kv = jnp.concatenate([keys, values], axis=0)
    kv_from = [passed_along(kv, "ctx", 2**m) for m in levels]
    q_from = [passed_along(queries, "ctx", -(2**m)) for m in levels]

    grad_att = lax.dot_general(
        lax.all_gather(d_out, "head", axis=1, tiled=True),
        out_weight,
        (((1,), (1,)), ((), ())),
        preferred_element_type=jnp.float32,
    )
    g = grad_att.astype(jnp.bfloat16)
    g_from = [passed_along(g, "ctx", -(2**m)) for m in levels]
    weight_cols = lax.all_to_all(out_weight, "head", 1, 0, tiled=True)
    kv_from, q_from, g_from, valid_q, valid_k, weight_cols = lax.optimization_barrier(
        (kv_from, q_from, g_from, valid_q, valid_k, weight_cols)
    )

    attended, query_grad, stats = query_call(
        valid_q, queries, g, keys, values, kv_from, heads_local, n_levels
    )
    output = projected(lax.all_gather(attended, "head", axis=1, tiled=True), weight_cols)

    st_from = [passed_along(stats, "ctx", -(2**m)) for m in levels]
    key_grad, value_grad = key_call(
        valid_k, keys, values, queries, g, stats, q_from, g_from, st_from, heads_local, n_levels
    )
    return output, query_grad, key_grad, value_grad


def solution(mesh):
    return jax.shard_map(
        local,
        mesh=mesh,
        in_specs=(
            P("ctx", "head"),
            P("ctx", "head"),
            P("ctx", "head"),
            P("head", None),
            P("ctx", "head"),
            P(),
            P(),
        ),
        out_specs=(P("ctx", "head"), P("ctx", "head"), P("ctx", "head"), P("ctx", "head")),
        check_vma=False,
    )
```
